128 devices in a mesh: img: 8 (over y, core), fsdp: 16 (over x, z).
Axes of the slice: x: 4, y: 4, z: 4, core: 2. Of those that a mesh axis runs over, the one named last changes fastest.
Arguments:
- text_states: bfloat16 [4096, 8192], P('img', 'fsdp'), may hold values from -100 to 100, as said below
- text_gain: float32 [8192], P('fsdp'), may hold values from 0.1 to 1.9
- gate_scale: float32 [8192], P('fsdp'), may hold values from 0.3 to 1.5
- live_counts: int32 [8], P('img'), may hold values from 1 to 512, 3072 in all
- token_slot: int32 [8, 512], P('img'), may hold values from 0 to 7, never falling along the last dimension, each value on 1 to 256 neighbouring positions
- wanted_images: int32 [8, 8], replicated, may hold values from 0 to 31, as said below
- patches: bfloat16 [32, 256, 1280], P('img', None, 'fsdp'), may hold values from -100 to 100, as said below
- latent_init: bfloat16 [64, 1280], replicated, may hold values from -100 to 100, as said below
- context_gain: float32 [1280], replicated, may hold values from 0.1 to 1.9
- latent_gain: float32 [1280], replicated, may hold values from 0.1 to 1.9
- res_query: bfloat16 [1280, 1536], P(None, 'fsdp'), may hold values from -0.15625 to 0.15625
- res_key: bfloat16 [1280, 1536], P(None, 'fsdp'), may hold values from -0.15625 to 0.15625
- res_value: bfloat16 [1280, 1536], P(None, 'fsdp'), may hold values from -0.15625 to 0.15625
- res_out: bfloat16 [1536, 1280], P('fsdp'), may hold values from -0.21875 to 0.21875
- final_gain: float32 [1280], P('fsdp'), may hold values from 0.1 to 1.9
- cross_query: bfloat16 [8192, 8192], P('fsdp'), may hold values from -0.09375 to 0.09375
- cross_key: bfloat16 [1280, 8192], P('fsdp'), may hold values from -0.25 to 0.25
- cross_value: bfloat16 [1280, 8192], P('fsdp'), may hold values from -0.25 to 0.25
- cross_out: bfloat16 [8192, 8192], P('fsdp'), may hold values from -0.09375 to 0.09375
Outputs:
- layer_output: float32 [4096, 8192], P('img', 'fsdp')
The draws below stay inside these ranges and needn't reach their ends.
Inputs may be any that keep to these rules, and one draw needn't show every extreme that they name: `wanted_images`: image i is held by owner i // 4 along img. A row lists 8 distinct images; every owner that appears in a row has exactly 2 of its images there. `token_slot`: along a shard's tokens the slot never falls, and every slot of the shard is used. Tokens of shard s at positions live_counts[s] and beyond are padding. `text_states`: real values. `patches`: real values. `latent_init`: real values.
All inputs are finite; a program needn't handle non-finite values.
Results may differ from the reference program's by a relative error of at most 0.0075.
Values may be sent and summed in bfloat16 or wider, within the bound.
No kernel may reach another device: no remote copies, remote signals or barrier semaphores. Data moves between devices by JAX's collectives and lax.ppermute only.
A program may use at most 128 MiB of HBM per device.

```python
import math
import jax
import jax.numpy as jnp
import numpy as np
from jax import lax

D = 8192
QH = 64
HEAD = 128
VIS = 1280
RH = 16
RHD = 96
R = 64
P_SIZE = 256
CAP = 8
PAIR = 2
IMG_DEV = 4
TOK_DEV = 512
HD = 8192
RINNER = 1536
SHARDS = 8
IMAGES = 32
TEXT = 4096
N_FSDP = 16


def scaled_field(field_key, row_total, col_total):
    first_key, second_key = jax.random.split(field_key, 2)
    col_pos = jnp.arange(col_total, dtype=jnp.float32) / col_total
    row_pos = jax.random.uniform(second_key, (row_total, 1), dtype=jnp.float32)
    noise_base = jnp.clip(jax.random.normal(first_key, (row_total, col_total), dtype=jnp.float32), -6.0, 6.0)
    field_scale = 10.0 ** (col_pos + row_pos - 1.0)
    return noise_base * field_scale


def draw_text_states(key, part):
    return scaled_field(jax.random.fold_in(key, 11), TEXT, D).astype(jnp.bfloat16)


def draw_patches(key, part):
    field = scaled_field(jax.random.fold_in(key, 12), IMAGES * P_SIZE, VIS)
    return field.reshape(IMAGES, P_SIZE, VIS).astype(jnp.bfloat16)


def draw_latent_init(key, part):
    return scaled_field(jax.random.fold_in(key, 13), R, VIS).astype(jnp.bfloat16)


def draw_wanted_images(key, part):
    base_key = jax.random.fold_in(key, 14)

    def one_shard(shard_key):
        owner_key, pick_key, order_key = jax.random.split(shard_key, 3)
        owners = jax.random.permutation(owner_key, SHARDS)[:CAP // PAIR]
        pick_keys = jax.random.split(pick_key, CAP // PAIR)
        picks = jax.vmap(lambda inner_key: jax.random.permutation(inner_key, IMG_DEV)[:PAIR])(pick_keys)
        listed = (owners[:, None] * IMG_DEV + picks).reshape(CAP)
        return jax.random.permutation(order_key, listed)
    return jax.vmap(one_shard)(jax.random.split(base_key, SHARDS)).astype(jnp.int32)


def with_spikes(entries, own_key, source, target, parts, factor):
    def block_of(dim):
        return (jnp.arange(entries.shape[dim]) // (entries.shape[dim] // parts)).reshape((-1,) + (1,) * (entries.ndim - 1 - dim))

    first = jax.random.permutation(own_key, parts)[block_of(target)]
    far = (block_of(target) + parts // 2) % parts
    return jnp.where((block_of(source) == first) | (block_of(source) == far), factor * entries, entries)


def block_scale(stream_key, extent, cuts, low, largest):
    loudness, own = 1.0, jax.random.fold_in(stream_key, 6)
    for dim, parts in cuts:
        steps = jnp.exp(jax.random.uniform(jax.random.fold_in(own, dim), (parts,), jnp.float32, low / len(cuts), largest / len(cuts)))
        loudness = loudness * jnp.repeat(steps, extent[dim] // parts).reshape([-1 if axis == dim else 1 for axis in range(len(extent))])
    return loudness


def length_profile(number_of, total, limit, lean):
    loads = [(1 << 20) // math.isqrt(grade ** lean) + 1 for grade in range(2, number_of + 1)]
    spare, counts = total - limit - (number_of - 1), [1] * (number_of - 1)
    while spare > 0:
        candidates = [i for i in range(number_of - 1) if counts[i] < limit]
        mass, remaining = sum([loads[i] for i in candidates]), spare
        for i in candidates:
            more = min(limit - counts[i], max(1, remaining * loads[i] // mass), spare)
            counts[i] = counts[i] + more
            spare = spare - more
    return np.array([limit] + counts)


def ragged(rng, amount, total, reach, skew):
    if amount == 2:
        one = jax.random.randint(rng, (), max(1, total - reach), min(reach, total - 1) + 1)
        return jnp.stack([one, total - one])
    lengths = jnp.asarray(length_profile(amount, total, reach, skew), jnp.int32)
    couples = (amount - 1) // 2
    source_of, taker = lengths[1:1 + 2 * couples:2], lengths[2:2 + 2 * couples:2]
    slack = jnp.minimum(source_of - 1, reach - taker)
    moved = jax.random.randint(jax.random.fold_in(rng, 1), (couples,), 0, 1 << 20) % (slack + 1)
    lengths = lengths.at[1:1 + 2 * couples:2].set(source_of - moved).at[2:2 + 2 * couples:2].set(taker + moved)
    return lengths[jax.random.permutation(jax.random.fold_in(rng, 2), amount)]


def scatter_about(own_key, shape, scale, limit, cuts=(), kind=jnp.bfloat16):
    drawn = jax.random.normal(own_key, shape, jnp.float32) * scale
    if len(cuts) > 0:
        drawn = block_scale(own_key, shape, cuts, -0.22, 0.18) * drawn
    return jnp.clip(drawn, min=-limit, max=limit).astype(kind)


def noise_with(stream_key, extent, scale, limit, shards, heavy, kind=jnp.bfloat16):
    values = scale * jax.random.normal(stream_key, extent, jnp.float32)
    if shards:
        values = values * block_scale(stream_key, extent, shards, -0.22, 0.18)
    return jnp.clip(with_spikes(values, jax.random.fold_in(stream_key, 3), *heavy), -limit, limit).astype(kind)


def setup_inputs(seed: int = 0) -> dict:
    streams_of = jax.random.split(jax.random.key(seed), 20)
    return {
        "text_states": draw_text_states(jax.random.fold_in(streams_of[19], 71), 0),
        "text_gain": jnp.clip(1.0 + 0.18 * jax.random.normal(streams_of[1], (D,), jnp.float32), 0.1, 1.9),
        "gate_scale": jnp.clip(0.3 + 1.2 * jax.random.uniform(streams_of[2], (D,), jnp.float32) ** block_scale(streams_of[2], (D,), ((0, 16),), -0.2, 0.2), 0.3, 1.5),
        "live_counts": ragged(streams_of[3], SHARDS, SHARDS * TOK_DEV * 3 // 4, TOK_DEV, 1).astype(jnp.int32),
        "token_slot": jax.vmap(lambda own: jnp.searchsorted(jnp.cumsum(ragged(own, CAP, TOK_DEV, TOK_DEV // 2, 1)), jnp.arange(TOK_DEV), side="right"))(jax.random.split(streams_of[4], SHARDS)).reshape((SHARDS, TOK_DEV)).astype(jnp.int32),
        "wanted_images": draw_wanted_images(jax.random.fold_in(streams_of[19], 71), 0),
        "patches": draw_patches(jax.random.fold_in(streams_of[19], 71), 0),
        "latent_init": draw_latent_init(jax.random.fold_in(streams_of[19], 71), 0),
        "context_gain": jnp.clip(1.0 + 0.18 * jax.random.normal(streams_of[8], (VIS,), jnp.float32), 0.1, 1.9),
        "latent_gain": jnp.clip(1.0 + 0.18 * jax.random.normal(streams_of[9], (VIS,), jnp.float32), 0.1, 1.9),
        "res_query": scatter_about(streams_of[10], (VIS, RINNER), VIS ** -0.5, 0.15625, ((1, 16),)),
        "res_key": scatter_about(streams_of[11], (VIS, RINNER), VIS ** -0.5, 0.15625, ((1, 16),)),
        "res_value": scatter_about(streams_of[12], (VIS, RINNER), VIS ** -0.5, 0.15625, ((1, 16),)),
        "res_out": noise_with(streams_of[13], (RINNER, VIS), RINNER ** -0.5, 0.21875, ((0, 16),), (0, 1, 16, 2.0)),
        "final_gain": jnp.clip(1.0 + 0.18 * jax.random.normal(streams_of[14], (VIS,), jnp.float32), 0.1, 1.9),
        "cross_query": noise_with(streams_of[15], (D, HD), D ** -0.5, 0.09375, ((0, 16),), (0, 1, 16, 2.0)),
        "cross_key": noise_with(streams_of[16], (VIS, HD), VIS ** -0.5, 0.25, ((0, 16),), (0, 1, 16, 2.0)),
        "cross_value": noise_with(streams_of[17], (VIS, HD), VIS ** -0.5, 0.25, ((0, 16),), (0, 1, 16, 2.0)),
        "cross_out": noise_with(streams_of[18], (HD, D), HD ** -0.5, 0.09375, ((0, 16),), (0, 1, 16, 2.0)),
    }


eps_norm = 1e-05
eps_rms = 1e-06

def layer_norm(values, gain_vec):
    values = values.astype(jnp.float32)
    row_mean = lax.optimization_barrier(jnp.mean(values, -1, keepdims=True))
    spread = lax.optimization_barrier(jnp.mean(values * values, -1, keepdims=True)) - row_mean * row_mean
    return (values - row_mean) * lax.rsqrt(spread + eps_norm) * gain_vec

def block_sum(left, right, blocks):
    block_width = left.shape[1] // blocks
    running = jnp.zeros((left.shape[0], right.shape[1]), jnp.float32)
    for block in range(blocks):
        lower = block * block_width
        product = jnp.dot(left[:, lower:lower + block_width], right[lower:lower + block_width], preferred_element_type=jnp.float32)
        running = running + lax.optimization_barrier(product.astype(jnp.bfloat16)).astype(jnp.float32)
    return running

def reference(text_states, text_gain, gate_scale, live_counts, token_slot, wanted_images, patches, latent_init, context_gain, latent_gain, res_query, res_key, res_value, res_out, final_gain, cross_query, cross_key, cross_value, cross_out):
    context = layer_norm(patches, context_gain).astype(jnp.bfloat16)
    latent_normed = layer_norm(latent_init, latent_gain).astype(jnp.bfloat16)
    res_q_rows = jnp.dot(latent_normed, res_query, preferred_element_type=jnp.float32).astype(jnp.bfloat16)
    query_split = res_q_rows.reshape(R, RH, RHD).astype(jnp.float32)
    res_scale = RHD ** (-0.5)

    def resample(image_rows):
        joined = jnp.concatenate([image_rows, latent_normed], 0)
        key_rows = jnp.dot(joined, res_key, preferred_element_type=jnp.float32).astype(jnp.bfloat16)
        value_rows = jnp.dot(joined, res_value, preferred_element_type=jnp.float32).astype(jnp.bfloat16)
        key_rows = key_rows.reshape(P_SIZE + R, RH, RHD).astype(jnp.float32)
        value_rows = value_rows.reshape(P_SIZE + R, RH, RHD).astype(jnp.float32)
        scores = jnp.einsum('rhe,khe->hrk', query_split, key_rows) * res_scale
        weights = jnp.exp(scores)
        weights = (weights / lax.optimization_barrier(jnp.sum(weights, -1, keepdims=True))).astype(jnp.bfloat16)
        mixed = jnp.einsum('hrk,khe->rhe', weights.astype(jnp.float32), value_rows)
        return mixed.astype(jnp.bfloat16).reshape(R, RINNER)
    mixed_all = lax.map(resample, context)
    mixed_proj = jnp.dot(mixed_all.reshape(IMAGES * R, RINNER), res_out, preferred_element_type=jnp.float32)
    latents = latent_init.astype(jnp.float32)[None] + mixed_proj.reshape(IMAGES, R, VIS)
    resampled = layer_norm(latents, final_gain).astype(jnp.bfloat16)
    text_f = text_states.astype(jnp.float32)
    normed = (text_f * lax.rsqrt(lax.optimization_barrier(jnp.mean(text_f * text_f, -1, keepdims=True)) + eps_rms) * text_gain).astype(jnp.bfloat16)
    query_all = block_sum(normed, cross_query, N_FSDP).astype(jnp.bfloat16)
    flat_latents = resampled.reshape(IMAGES * R, VIS)
    key_all = block_sum(flat_latents, cross_key, N_FSDP).astype(jnp.bfloat16).reshape(IMAGES, R, QH, HEAD)
    value_all = block_sum(flat_latents, cross_value, N_FSDP).astype(jnp.bfloat16).reshape(IMAGES, R, QH, HEAD)
    cross_scale = HEAD ** (-0.5)

    def attend(shard_inputs):
        shard_query, shard_slots, shard_images = shard_inputs
        slot_keys = key_all[shard_images].astype(jnp.float32)
        slot_values = value_all[shard_images].astype(jnp.float32)
        query_heads = shard_query.reshape(TOK_DEV, QH, HEAD).astype(jnp.float32)
        scores = jnp.einsum('the,crhe->htcr', query_heads, slot_keys) * cross_scale
        slot_hot = (shard_slots[:, None] == jnp.arange(CAP, dtype=jnp.int32)[None, :]).astype(jnp.float32)
        weights = jnp.exp(scores) * slot_hot[None, :, :, None]
        weights = (weights / lax.optimization_barrier(jnp.sum(weights, axis=(2, 3), keepdims=True))).astype(jnp.bfloat16)
        mixed = jnp.einsum('htcr,crhe->the', weights.astype(jnp.float32), slot_values)
        return mixed.astype(jnp.bfloat16).reshape(TOK_DEV, HD)
    attended = lax.map(attend, (query_all.reshape(SHARDS, TOK_DEV, HD), token_slot, wanted_images)).reshape(TEXT, HD)
    projected = block_sum(attended, cross_out, N_FSDP)
    positions = jnp.arange(TOK_DEV, dtype=jnp.int32)
    live_mask = (positions[None, :] < live_counts[:, None]).astype(jnp.float32).reshape(TEXT, 1)
    return text_f + jnp.tanh(gate_scale) * projected * live_mask
```

```python
import jax
import jax.numpy as jnp
from jax import lax
from jax.sharding import PartitionSpec as P

D = 8192
HEAD = 128
RHD = 96
PAIR = 2


eps_norm = 1e-05
eps_rms = 1e-06


def layer_norm(values, gain_vec):
    values = values.astype(jnp.float32)
    row_mean = jnp.mean(values, -1, keepdims=True)
    spread = jnp.mean(values * values, -1, keepdims=True) - row_mean * row_mean
    return (values - row_mean) * lax.rsqrt(spread + eps_norm) * gain_vec


def route_tables(wanted_images, per_owner, pair_slots):
    owners = wanted_images // per_owner
    slot_total = wanted_images.shape[1]
    positions = jnp.arange(slot_total, dtype=jnp.int32)
    before = (owners[:, :, None] == owners[:, None, :]) & (
        positions[None, None, :] < positions[None, :, None]
    )
    slot_rank = jnp.sum(before.astype(jnp.int32), axis=2)
    rank_hot = (
        slot_rank[:, :, None] == jnp.arange(pair_slots, dtype=jnp.int32)[None, None, :]
    ).astype(jnp.float32)
    return (owners, rank_hot)


def pack_rows(row_data, wanted_images, my_shard, per_owner, pair_slots):
    owners, rank_hot = route_tables(wanted_images, per_owner, pair_slots)
    is_mine = (owners == my_shard).astype(jnp.float32)
    local_hot = (
        (wanted_images % per_owner)[:, :, None]
        == jnp.arange(per_owner, dtype=jnp.int32)[None, None, :]
    ).astype(jnp.float32)
    picker = jnp.einsum("scp,sci->spi", rank_hot * is_mine[:, :, None], local_hot).astype(
        jnp.bfloat16
    )
    return jnp.einsum("spi,if->spf", picker, row_data, preferred_element_type=jnp.float32).astype(
        jnp.bfloat16
    )


def unpack_rows(received, wanted_images, my_shard, per_owner, pair_slots):
    owners, rank_hot = route_tables(wanted_images, per_owner, pair_slots)
    owner_row = lax.dynamic_slice_in_dim(owners, my_shard, 1, 0)[0]
    rank_row = lax.dynamic_slice_in_dim(rank_hot, my_shard, 1, 0)[0]
    source_hot = (
        owner_row[:, None] == jnp.arange(received.shape[0], dtype=jnp.int32)[None, :]
    ).astype(jnp.float32)
    taker = (source_hot[:, :, None] * rank_row[:, None, :]).astype(jnp.bfloat16)
    return jnp.einsum("cop,opf->cf", taker, received, preferred_element_type=jnp.float32).astype(
        jnp.bfloat16
    )


def gather_blocks(block, axis_name, parts):
    spread = jnp.broadcast_to(block[None], (parts,) + block.shape)
    return lax.all_to_all(spread, axis_name, split_axis=0, concat_axis=0, tiled=True)


def block_dot(rows, cols):
    contracted = jnp.einsum("brk,bkc->brc", rows, cols, preferred_element_type=jnp.float32)
    rounded = lax.reduce_precision(contracted, exponent_bits=8, mantissa_bits=7)
    return jnp.sum(rounded, 0)


def local(
    text_states,
    text_gain,
    gate_scale,
    live_counts,
    token_slot,
    wanted_images,
    patches,
    latent_init,
    context_gain,
    latent_gain,
    res_query,
    res_key,
    res_value,
    res_out,
    final_gain,
    cross_query,
    cross_key,
    cross_value,
    cross_out,
):
    my_feature = lax.axis_index("fsdp")
    my_shard = lax.axis_index("img")
    parts = lax.axis_size("fsdp")
    image_count = patches.shape[0]
    patch_count = patches.shape[1]
    feat_vis = patches.shape[2]
    latent_count = latent_init.shape[0]
    vis_width = latent_init.shape[1]
    res_cols = res_query.shape[1]
    res_heads = res_cols // RHD
    head_cols = cross_out.shape[0]
    token_count = text_states.shape[0]
    slot_count = wanted_images.shape[1]
    cross_heads = head_cols // HEAD
    contract_first = (((0,), (1,)), ((), ()))
    kv_weights = jnp.stack([cross_key, cross_value], 0).reshape(2, feat_vis, parts, head_cols)
    kv_weights = lax.all_to_all(
        jnp.transpose(kv_weights, (2, 0, 1, 3)), "fsdp", split_axis=0, concat_axis=0, tiled=True
    )
    text_f = text_states.astype(jnp.float32)
    squares = jnp.sum(gather_blocks(jnp.sum(text_f * text_f, -1), "fsdp", parts), 0)
    normed = (text_f * lax.rsqrt(squares / D + eps_rms)[:, None] * text_gain).astype(jnp.bfloat16)
    query_cols = lax.psum_scatter(
        lax.dot_general(
            cross_query, normed, contract_first, preferred_element_type=jnp.float32
        ).astype(jnp.bfloat16),
        "fsdp",
        scatter_dimension=0,
        tiled=True,
    )
    full_patches = lax.all_gather(patches, "fsdp", axis=2, tiled=True)
    context = layer_norm(full_patches, context_gain).astype(jnp.bfloat16)
    latent_normed = layer_norm(latent_init, latent_gain).astype(jnp.bfloat16)
    res_q_rows = jnp.dot(latent_normed, res_query, preferred_element_type=jnp.float32).astype(
        jnp.bfloat16
    )
    res_q_rows = res_q_rows.reshape(latent_count, res_heads, RHD)
    ctx_keys = jnp.einsum(
        "npv,vk->npk", context, res_key, preferred_element_type=jnp.float32
    ).astype(jnp.bfloat16)
    ctx_values = jnp.einsum(
        "npv,vk->npk", context, res_value, preferred_element_type=jnp.float32
    ).astype(jnp.bfloat16)
    lat_keys = jnp.dot(latent_normed, res_key, preferred_element_type=jnp.float32).astype(
        jnp.bfloat16
    )
    lat_values = jnp.dot(latent_normed, res_value, preferred_element_type=jnp.float32).astype(
        jnp.bfloat16
    )
    joined_shape = (image_count, latent_count, res_cols)
    key_rows = jnp.concatenate([ctx_keys, jnp.broadcast_to(lat_keys[None], joined_shape)], 1)
    value_rows = jnp.concatenate([ctx_values, jnp.broadcast_to(lat_values[None], joined_shape)], 1)
    key_rows = key_rows.reshape(image_count, patch_count + latent_count, res_heads, RHD)
    value_rows = value_rows.reshape(image_count, patch_count + latent_count, res_heads, RHD)
    res_scores = jnp.einsum(
        "rhe,nkhe->nhrk", res_q_rows, key_rows, preferred_element_type=jnp.float32
    ) * RHD ** (-0.5)
    res_weights = jnp.exp(res_scores)
    res_weights = (res_weights / jnp.sum(res_weights, -1, keepdims=True)).astype(jnp.bfloat16)
    res_mixed = jnp.einsum(
        "nhrk,nkhe->nrhe", res_weights, value_rows, preferred_element_type=jnp.float32
    )
    res_mixed = res_mixed.astype(jnp.bfloat16).reshape(image_count * latent_count, res_cols)
    row_total = image_count * latent_count
    row_part = row_total // parts
    head_part = jnp.dot(res_mixed, res_out, preferred_element_type=jnp.float32).astype(jnp.bfloat16)
    head_part = lax.all_to_all(
        head_part.reshape(parts, row_part, vis_width), "fsdp", split_axis=0, concat_axis=0, tiled=True
    )
    my_rows = my_feature * row_part
    init_rows = lax.dynamic_slice_in_dim(latent_init, my_rows % latent_count, row_part, 0)
    latents = init_rows.astype(jnp.float32) + jnp.sum(head_part.astype(jnp.float32), 0)
    full_gain = gather_blocks(final_gain, "fsdp", parts).reshape(vis_width)
    resampled_rows = layer_norm(latents, full_gain).astype(jnp.bfloat16)
    resampled = lax.all_to_all(
        jnp.transpose(resampled_rows.reshape(row_part, parts, feat_vis), (1, 0, 2)),
        "fsdp",
        split_axis=0,
        concat_axis=0,
        tiled=True,
    )
    per_image = resampled.reshape(image_count, latent_count * feat_vis)
    outgoing = pack_rows(per_image, wanted_images, my_shard, image_count, PAIR)
    incoming = lax.all_to_all(outgoing, "img", split_axis=0, concat_axis=0, tiled=True)
    slot_latents = unpack_rows(incoming, wanted_images, my_shard, image_count, PAIR).reshape(
        slot_count * latent_count, feat_vis
    )
    slot_blocks = gather_blocks(slot_latents, "fsdp", parts)
    slot_keys = block_dot(slot_blocks, kv_weights[:, 0]).astype(jnp.bfloat16)
    slot_values = block_dot(slot_blocks, kv_weights[:, 1]).astype(jnp.bfloat16)
    slot_keys = slot_keys.reshape(slot_count, latent_count, cross_heads, HEAD)
    slot_values = slot_values.reshape(slot_count, latent_count, cross_heads, HEAD)
    query_heads = query_cols.reshape(cross_heads, HEAD, token_count)
    scores = jnp.einsum(
        "het,crhe->htcr", query_heads, slot_keys, preferred_element_type=jnp.float32
    ) * HEAD ** (-0.5)
    slot_hot = (token_slot[0][:, None] == jnp.arange(slot_count, dtype=jnp.int32)[None, :]).astype(
        jnp.float32
    )
    weights = jnp.exp(scores) * slot_hot[None, :, :, None]
    weights = (weights / jnp.sum(weights, axis=(2, 3), keepdims=True)).astype(jnp.bfloat16)
    attended = jnp.einsum(
        "htcr,crhe->het", weights, slot_values, preferred_element_type=jnp.float32
    )
    attended = attended.astype(jnp.bfloat16).reshape(head_cols, token_count)
    projected_cols = lax.psum_scatter(
        lax.dot_general(
            cross_out, attended, (((0,), (0,)), ((), ())), preferred_element_type=jnp.float32
        ).astype(jnp.bfloat16),
        "fsdp",
        scatter_dimension=0,
        tiled=True,
    ).astype(jnp.float32)
    projected = jnp.transpose(projected_cols)
    positions = jnp.arange(token_count, dtype=jnp.int32)
    live_mask = (positions < live_counts[0]).astype(jnp.float32)[:, None]
    return text_f + jnp.tanh(gate_scale) * projected * live_mask


def solution(mesh):
    placed = (
        P("img", "fsdp"),
        P("fsdp"),
        P("fsdp"),
        P("img"),
        P("img", None),
        P(),
        P("img", None, "fsdp"),
        P(),
        P(),
        P(),
        P(None, "fsdp"),
        P(None, "fsdp"),
        P(None, "fsdp"),
        P("fsdp", None),
        P("fsdp"),
        P("fsdp", None),
        P("fsdp", None),
        P("fsdp", None),
        P("fsdp", None),
    )
    return jax.shard_map(
        local, mesh=mesh, in_specs=placed, out_specs=P("img", "fsdp"), check_vma=False
    )
```

```python
import jax
import jax.numpy as jnp
from jax import lax
from jax.sharding import PartitionSpec as P

D = 8192
HEAD = 128
RHD = 96
PAIR = 2


eps_norm = 1e-05
eps_rms = 1e-06


def layer_norm(values, gain_vec):
    values = values.astype(jnp.float32)
    row_mean = jnp.mean(values, -1, keepdims=True)
    spread = jnp.mean(values * values, -1, keepdims=True) - row_mean * row_mean
    return (values - row_mean) * lax.rsqrt(spread + eps_norm) * gain_vec


def route_tables(wanted_images, per_owner, pair_slots):
    owners = wanted_images // per_owner
    slot_total = wanted_images.shape[1]
    positions = jnp.arange(slot_total, dtype=jnp.int32)
    before = (owners[:, :, None] == owners[:, None, :]) & (
        positions[None, None, :] < positions[None, :, None]
    )
    slot_rank = jnp.sum(before.astype(jnp.int32), axis=2)
    rank_hot = (
        slot_rank[:, :, None] == jnp.arange(pair_slots, dtype=jnp.int32)[None, None, :]
    ).astype(jnp.float32)
    return (owners, rank_hot)


def pack_rows(row_data, wanted_images, my_shard, per_owner, pair_slots):
    owners, rank_hot = route_tables(wanted_images, per_owner, pair_slots)
    is_mine = (owners == my_shard).astype(jnp.float32)
    local_hot = (
        (wanted_images % per_owner)[:, :, None]
        == jnp.arange(per_owner, dtype=jnp.int32)[None, None, :]
    ).astype(jnp.float32)
    picker = jnp.einsum("scp,sci->spi", rank_hot * is_mine[:, :, None], local_hot).astype(
        jnp.bfloat16
    )
    return jnp.einsum("spi,if->spf", picker, row_data, preferred_element_type=jnp.float32).astype(
        jnp.bfloat16
    )


def unpack_rows(received, wanted_images, my_shard, per_owner, pair_slots):
    owners, rank_hot = route_tables(wanted_images, per_owner, pair_slots)
    owner_row = lax.dynamic_slice_in_dim(owners, my_shard, 1, 0)[0]
    rank_row = lax.dynamic_slice_in_dim(rank_hot, my_shard, 1, 0)[0]
    source_hot = (
        owner_row[:, None] == jnp.arange(received.shape[0], dtype=jnp.int32)[None, :]
    ).astype(jnp.float32)
    taker = (source_hot[:, :, None] * rank_row[:, None, :]).astype(jnp.bfloat16)
    return jnp.einsum("cop,opf->cf", taker, received, preferred_element_type=jnp.float32).astype(
        jnp.bfloat16
    )


def gather_blocks(block, axis_name, parts):
    spread = jnp.broadcast_to(block[None], (parts,) + block.shape)
    return lax.all_to_all(spread, axis_name, split_axis=0, concat_axis=0, tiled=True)


def block_dot(rows, cols):
    contracted = jnp.einsum("brk,bkc->brc", rows, cols, preferred_element_type=jnp.float32)
    rounded = lax.reduce_precision(contracted, exponent_bits=8, mantissa_bits=7)
    return jnp.sum(rounded, 0)


def local(
    text_states,
    text_gain,
    gate_scale,
    live_counts,
    token_slot,
    wanted_images,
    patches,
    latent_init,
    context_gain,
    latent_gain,
    res_query,
    res_key,
    res_value,
    res_out,
    final_gain,
    cross_query,
    cross_key,
    cross_value,
    cross_out,
):
    my_feature = lax.axis_index("fsdp")
    my_shard = lax.axis_index("img")
    parts = lax.axis_size("fsdp")
    image_count = patches.shape[0]
    patch_count = patches.shape[1]
    feat_vis = patches.shape[2]
    latent_count = latent_init.shape[0]
    vis_width = latent_init.shape[1]
    res_cols = res_query.shape[1]
    res_heads = res_cols // RHD
    head_cols = cross_out.shape[0]
    token_count = text_states.shape[0]
    slot_count = wanted_images.shape[1]
    cross_heads = head_cols // HEAD
    contract_first = (((0,), (1,)), ((), ()))
    kv_stack = jnp.stack([cross_key, cross_value], 0)
    kv_blocks = []
    for shift in range(parts):
        dest_cols = ((my_feature + shift) % parts) * head_cols
        block = lax.dynamic_slice_in_dim(kv_stack, dest_cols, head_cols, 2)
        if shift:
            ring = [(j, (j + shift) % parts) for j in range(parts)]
            block = lax.ppermute(block, "fsdp", ring)
        kv_blocks.append(block)
    kv_weights = jnp.stack(kv_blocks, 0)
    block_source = (my_feature - jnp.arange(parts, dtype=jnp.int32)) % parts
    text_f = text_states.astype(jnp.float32)
    squares = jnp.sum(gather_blocks(jnp.sum(text_f * text_f, -1), "fsdp", parts), 0)
    normed = (text_f * lax.rsqrt(squares / D + eps_rms)[:, None] * text_gain).astype(jnp.bfloat16)
    query_cols = lax.psum_scatter(
        lax.dot_general(
            cross_query, normed, contract_first, preferred_element_type=jnp.float32
        ).astype(jnp.bfloat16),
        "fsdp",
        scatter_dimension=0,
        tiled=True,
    )
    full_patches = lax.all_gather(patches, "fsdp", axis=2, tiled=True)
    context = layer_norm(full_patches, context_gain).astype(jnp.bfloat16)
    latent_normed = layer_norm(latent_init, latent_gain).astype(jnp.bfloat16)
    res_q_rows = jnp.dot(latent_normed, res_query, preferred_element_type=jnp.float32).astype(
        jnp.bfloat16
    )
    res_q_rows = res_q_rows.reshape(latent_count, res_heads, RHD)
    ctx_keys = jnp.einsum(
        "npv,vk->npk", context, res_key, preferred_element_type=jnp.float32
    ).astype(jnp.bfloat16)
    ctx_values = jnp.einsum(
        "npv,vk->npk", context, res_value, preferred_element_type=jnp.float32
    ).astype(jnp.bfloat16)
    lat_keys = jnp.dot(latent_normed, res_key, preferred_element_type=jnp.float32).astype(
        jnp.bfloat16
    )
    lat_values = jnp.dot(latent_normed, res_value, preferred_element_type=jnp.float32).astype(
        jnp.bfloat16
    )
    joined_shape = (image_count, latent_count, res_cols)
    key_rows = jnp.concatenate([ctx_keys, jnp.broadcast_to(lat_keys[None], joined_shape)], 1)
    value_rows = jnp.concatenate([ctx_values, jnp.broadcast_to(lat_values[None], joined_shape)], 1)
    key_rows = key_rows.reshape(image_count, patch_count + latent_count, res_heads, RHD)
    value_rows = value_rows.reshape(image_count, patch_count + latent_count, res_heads, RHD)
    res_scores = jnp.einsum(
        "rhe,nkhe->nhrk", res_q_rows, key_rows, preferred_element_type=jnp.float32
    ) * RHD ** (-0.5)
    res_weights = jnp.exp(res_scores)
    res_weights = (res_weights / jnp.sum(res_weights, -1, keepdims=True)).astype(jnp.bfloat16)
    res_mixed = jnp.einsum(
        "nhrk,nkhe->nrhe", res_weights, value_rows, preferred_element_type=jnp.float32
    )
    res_mixed = res_mixed.astype(jnp.bfloat16).reshape(image_count * latent_count, res_cols)
    row_total = image_count * latent_count
    row_part = row_total // parts
    head_part = jnp.dot(res_mixed, res_out, preferred_element_type=jnp.float32).astype(jnp.bfloat16)
    head_part = lax.all_to_all(
        head_part.reshape(parts, row_part, vis_width), "fsdp", split_axis=0, concat_axis=0, tiled=True
    )
    my_rows = my_feature * row_part
    init_rows = lax.dynamic_slice_in_dim(latent_init, my_rows % latent_count, row_part, 0)
    latents = init_rows.astype(jnp.float32) + jnp.sum(head_part.astype(jnp.float32), 0)
    full_gain = gather_blocks(final_gain, "fsdp", parts).reshape(vis_width)
    resampled_rows = layer_norm(latents, full_gain).astype(jnp.bfloat16)
    resampled = lax.all_to_all(
        jnp.transpose(resampled_rows.reshape(row_part, parts, feat_vis), (1, 0, 2)),
        "fsdp",
        split_axis=0,
        concat_axis=0,
        tiled=True,
    )
    per_image = resampled.reshape(image_count, latent_count * feat_vis)
    outgoing = pack_rows(per_image, wanted_images, my_shard, image_count, PAIR)
    incoming = lax.all_to_all(outgoing, "img", split_axis=0, concat_axis=0, tiled=True)
    slot_latents = unpack_rows(incoming, wanted_images, my_shard, image_count, PAIR).reshape(
        slot_count * latent_count, feat_vis
    )
    slot_blocks = jnp.take(gather_blocks(slot_latents, "fsdp", parts), block_source, axis=0)
    slot_keys = block_dot(slot_blocks, kv_weights[:, 0]).astype(jnp.bfloat16)
    slot_values = block_dot(slot_blocks, kv_weights[:, 1]).astype(jnp.bfloat16)
    slot_keys = slot_keys.reshape(slot_count, latent_count, cross_heads, HEAD)
    slot_values = slot_values.reshape(slot_count, latent_count, cross_heads, HEAD)
    query_heads = query_cols.reshape(cross_heads, HEAD, token_count)
    scores = jnp.einsum(
        "het,crhe->htcr", query_heads, slot_keys, preferred_element_type=jnp.float32
    ) * HEAD ** (-0.5)
    slot_hot = (token_slot[0][:, None] == jnp.arange(slot_count, dtype=jnp.int32)[None, :]).astype(
        jnp.float32
    )
    weights = jnp.exp(scores) * slot_hot[None, :, :, None]
    weights = (weights / jnp.sum(weights, axis=(2, 3), keepdims=True)).astype(jnp.bfloat16)
    attended = jnp.einsum(
        "htcr,crhe->het", weights, slot_values, preferred_element_type=jnp.float32
    )
    attended = attended.astype(jnp.bfloat16).reshape(head_cols, token_count)
    projected_cols = lax.psum_scatter(
        lax.dot_general(
            cross_out, attended, (((0,), (0,)), ((), ())), preferred_element_type=jnp.float32
        ).astype(jnp.bfloat16),
        "fsdp",
        scatter_dimension=0,
        tiled=True,
    ).astype(jnp.float32)
    projected = jnp.transpose(projected_cols)
    positions = jnp.arange(token_count, dtype=jnp.int32)
    live_mask = (positions < live_counts[0]).astype(jnp.float32)[:, None]
    return text_f + jnp.tanh(gate_scale) * projected * live_mask


def solution(mesh):
    placed = (
        P("img", "fsdp"),
        P("fsdp"),
        P("fsdp"),
        P("img"),
        P("img", None),
        P(),
        P("img", None, "fsdp"),
        P(),
        P(),
        P(),
        P(None, "fsdp"),
        P(None, "fsdp"),
        P(None, "fsdp"),
        P("fsdp", None),
        P("fsdp"),
        P("fsdp", None),
        P("fsdp", None),
        P("fsdp", None),
        P("fsdp", None),
    )
    return jax.shard_map(
        local, mesh=mesh, in_specs=placed, out_specs=P("img", "fsdp"), check_vma=False
    )
```

```python
import jax
import jax.numpy as jnp
from jax import lax
from jax.sharding import PartitionSpec as P

D = 8192
HEAD = 128
RHD = 96
PAIR = 2


eps_norm = 1e-05
eps_rms = 1e-06


def layer_norm(values, gain_vec):
    values = values.astype(jnp.float32)
    row_mean = jnp.mean(values, -1, keepdims=True)
    spread = jnp.mean(values * values, -1, keepdims=True) - row_mean * row_mean
    return (values - row_mean) * lax.rsqrt(spread + eps_norm) * gain_vec


def route_tables(wanted_images, per_owner, pair_slots):
    owners = wanted_images // per_owner
    slot_total = wanted_images.shape[1]
    positions = jnp.arange(slot_total, dtype=jnp.int32)
    before = (owners[:, :, None] == owners[:, None, :]) & (
        positions[None, None, :] < positions[None, :, None]
    )
    slot_rank = jnp.sum(before.astype(jnp.int32), axis=2)
    rank_hot = (
        slot_rank[:, :, None] == jnp.arange(pair_slots, dtype=jnp.int32)[None, None, :]
    ).astype(jnp.float32)
    return (owners, rank_hot)


def pack_rows(row_data, wanted_images, my_shard, per_owner, pair_slots):
    owners, rank_hot = route_tables(wanted_images, per_owner, pair_slots)
    is_mine = (owners == my_shard).astype(jnp.float32)
    local_hot = (
        (wanted_images % per_owner)[:, :, None]
        == jnp.arange(per_owner, dtype=jnp.int32)[None, None, :]
    ).astype(jnp.float32)
    picker = jnp.einsum("scp,sci->spi", rank_hot * is_mine[:, :, None], local_hot).astype(
        jnp.bfloat16
    )
    return jnp.einsum("spi,if->spf", picker, row_data, preferred_element_type=jnp.float32).astype(
        jnp.bfloat16
    )


def unpack_rows(received, wanted_images, my_shard, per_owner, pair_slots):
    owners, rank_hot = route_tables(wanted_images, per_owner, pair_slots)
    owner_row = lax.dynamic_slice_in_dim(owners, my_shard, 1, 0)[0]
    rank_row = lax.dynamic_slice_in_dim(rank_hot, my_shard, 1, 0)[0]
    source_hot = (
        owner_row[:, None] == jnp.arange(received.shape[0], dtype=jnp.int32)[None, :]
    ).astype(jnp.float32)
    taker = (source_hot[:, :, None] * rank_row[:, None, :]).astype(jnp.bfloat16)
    return jnp.einsum("cop,opf->cf", taker, received, preferred_element_type=jnp.float32).astype(
        jnp.bfloat16
    )


def gather_blocks(block, axis_name, parts):
    spread = jnp.broadcast_to(block[None], (parts,) + block.shape)
    return lax.all_to_all(spread, axis_name, split_axis=0, concat_axis=0, tiled=True)


def block_dot(rows, cols):
    contracted = jnp.einsum("brk,bkc->brc", rows, cols, preferred_element_type=jnp.float32)
    rounded = lax.reduce_precision(contracted, exponent_bits=8, mantissa_bits=7)
    return jnp.sum(rounded, 0)


def local(
    text_states,
    text_gain,
    gate_scale,
    live_counts,
    token_slot,
    wanted_images,
    patches,
    latent_init,
    context_gain,
    latent_gain,
    res_query,
    res_key,
    res_value,
    res_out,
    final_gain,
    cross_query,
    cross_key,
    cross_value,
    cross_out,
):
    my_feature = lax.axis_index("fsdp")
    my_shard = lax.axis_index("img")
    parts = lax.axis_size("fsdp")
    image_count = patches.shape[0]
    patch_count = patches.shape[1]
    feat_vis = patches.shape[2]
    latent_count = latent_init.shape[0]
    vis_width = latent_init.shape[1]
    res_cols = res_query.shape[1]
    res_heads = res_cols // RHD
    head_cols = cross_out.shape[0]
    token_count = text_states.shape[0]
    slot_count = wanted_images.shape[1]
    cross_heads = head_cols // HEAD
    contract_first = (((0,), (1,)), ((), ()))
    kv_stack = jnp.stack([cross_key, cross_value], 0)
    kv_blocks = []
    for shift in range(parts):
        dest_cols = ((my_feature + shift) % parts) * head_cols
        block = lax.dynamic_slice_in_dim(kv_stack, dest_cols, head_cols, 2)
        if shift:
            ring = [(j, (j + shift) % parts) for j in range(parts)]
            block = lax.ppermute(block, "fsdp", ring)
        kv_blocks.append(block)
    kv_weights = jnp.stack(kv_blocks, 0)
    block_source = (my_feature - jnp.arange(parts, dtype=jnp.int32)) % parts
    text_f = text_states.astype(jnp.float32)
    gained = (text_f * text_gain).astype(jnp.bfloat16)
    query_cols = lax.psum_scatter(
        lax.dot_general(
            cross_query, gained, contract_first, preferred_element_type=jnp.float32
        ).astype(jnp.bfloat16),
        "fsdp",
        scatter_dimension=0,
        tiled=True,
    )
    patch_blocks = gather_blocks(patches, "fsdp", parts)
    full_patches = jnp.transpose(patch_blocks, (1, 2, 0, 3)).reshape(
        image_count, patch_count, vis_width
    )
    context = layer_norm(full_patches, context_gain).astype(jnp.bfloat16)
    latent_normed = layer_norm(latent_init, latent_gain).astype(jnp.bfloat16)
    res_q_rows = jnp.dot(latent_normed, res_query, preferred_element_type=jnp.float32).astype(
        jnp.bfloat16
    )
    res_q_rows = res_q_rows.reshape(latent_count, res_heads, RHD)
    ctx_keys = jnp.einsum(
        "npv,vk->npk", context, res_key, preferred_element_type=jnp.float32
    ).astype(jnp.bfloat16)
    ctx_values = jnp.einsum(
        "npv,vk->npk", context, res_value, preferred_element_type=jnp.float32
    ).astype(jnp.bfloat16)
    lat_keys = jnp.dot(latent_normed, res_key, preferred_element_type=jnp.float32).astype(
        jnp.bfloat16
    )
    lat_values = jnp.dot(latent_normed, res_value, preferred_element_type=jnp.float32).astype(
        jnp.bfloat16
    )
    joined_shape = (image_count, latent_count, res_cols)
    key_rows = jnp.concatenate([ctx_keys, jnp.broadcast_to(lat_keys[None], joined_shape)], 1)
    value_rows = jnp.concatenate([ctx_values, jnp.broadcast_to(lat_values[None], joined_shape)], 1)
    key_rows = key_rows.reshape(image_count, patch_count + latent_count, res_heads, RHD)
    value_rows = value_rows.reshape(image_count, patch_count + latent_count, res_heads, RHD)
    res_scores = jnp.einsum(
        "rhe,nkhe->nhrk", res_q_rows, key_rows, preferred_element_type=jnp.float32
    ) * RHD ** (-0.5)
    res_weights = jnp.exp(res_scores)
    res_weights = (res_weights / jnp.sum(res_weights, -1, keepdims=True)).astype(jnp.bfloat16)
    res_mixed = jnp.einsum(
        "nhrk,nkhe->nrhe", res_weights, value_rows, preferred_element_type=jnp.float32
    )
    res_mixed = res_mixed.astype(jnp.bfloat16).reshape(image_count * latent_count, res_cols)
    stats = jnp.concatenate([jnp.sum(text_f * text_f, -1), final_gain], 0)
    stats = gather_blocks(stats, "fsdp", parts)
    squares = jnp.sum(stats[:, :token_count], 0)
    full_gain = stats[:, token_count:].reshape(vis_width)
    row_total = image_count * latent_count
    row_part = row_total // parts
    head_part = jnp.dot(res_mixed, res_out, preferred_element_type=jnp.float32).astype(jnp.bfloat16)
    head_part = lax.all_to_all(
        head_part.reshape(parts, row_part, vis_width), "fsdp", split_axis=0, concat_axis=0, tiled=True
    )
    my_rows = my_feature * row_part
    init_rows = lax.dynamic_slice_in_dim(latent_init, my_rows % latent_count, row_part, 0)
    latents = init_rows.astype(jnp.float32) + jnp.sum(head_part.astype(jnp.float32), 0)
    resampled_rows = layer_norm(latents, full_gain).astype(jnp.bfloat16)
    owner_rows = gather_blocks(resampled_rows, "fsdp", parts).reshape(row_total, parts, feat_vis)
    owner_blocks = jnp.take(jnp.transpose(owner_rows, (1, 0, 2)), block_source, axis=0)
    owner_keys = block_dot(owner_blocks, kv_weights[:, 0]).astype(jnp.bfloat16)
    owner_values = block_dot(owner_blocks, kv_weights[:, 1]).astype(jnp.bfloat16)
    owner_kv = jnp.concatenate(
        [
            owner_keys.reshape(image_count, latent_count, head_cols),
            owner_values.reshape(image_count, latent_count, head_cols),
        ],
        2,
    ).reshape(image_count, latent_count * 2 * head_cols)
    outgoing = pack_rows(owner_kv, wanted_images, my_shard, image_count, PAIR)
    incoming = lax.all_to_all(outgoing, "img", split_axis=0, concat_axis=0, tiled=True)
    slot_kv = unpack_rows(incoming, wanted_images, my_shard, image_count, PAIR).reshape(
        slot_count, latent_count, 2, cross_heads, HEAD
    )
    slot_keys = slot_kv[:, :, 0]
    slot_values = slot_kv[:, :, 1]
    token_scale = lax.rsqrt(squares / D + eps_rms)
    query_cols = (query_cols.astype(jnp.float32) * token_scale[None, :]).astype(jnp.bfloat16)
    query_heads = query_cols.reshape(cross_heads, HEAD, token_count)
    scores = jnp.einsum(
        "het,crhe->htcr", query_heads, slot_keys, preferred_element_type=jnp.float32
    ) * HEAD ** (-0.5)
    slot_hot = (token_slot[0][:, None] == jnp.arange(slot_count, dtype=jnp.int32)[None, :]).astype(
        jnp.float32
    )
    weights = jnp.exp(scores) * slot_hot[None, :, :, None]
    weights = (weights / jnp.sum(weights, axis=(2, 3), keepdims=True)).astype(jnp.bfloat16)
    attended = jnp.einsum(
        "htcr,crhe->het", weights, slot_values, preferred_element_type=jnp.float32
    )
    attended = attended.astype(jnp.bfloat16).reshape(head_cols, token_count)
    projected_cols = lax.psum_scatter(
        lax.dot_general(
            cross_out, attended, (((0,), (0,)), ((), ())), preferred_element_type=jnp.float32
        ).astype(jnp.bfloat16),
        "fsdp",
        scatter_dimension=0,
        tiled=True,
    ).astype(jnp.float32)
    projected = jnp.transpose(projected_cols)
    positions = jnp.arange(token_count, dtype=jnp.int32)
    live_mask = (positions < live_counts[0]).astype(jnp.float32)[:, None]
    return text_f + jnp.tanh(gate_scale) * projected * live_mask


def solution(mesh):
    placed = (
        P("img", "fsdp"),
        P("fsdp"),
        P("fsdp"),
        P("img"),
        P("img", None),
        P(),
        P("img", None, "fsdp"),
        P(),
        P(),
        P(),
        P(None, "fsdp"),
        P(None, "fsdp"),
        P(None, "fsdp"),
        P("fsdp", None),
        P("fsdp"),
        P("fsdp", None),
        P("fsdp", None),
        P("fsdp", None),
        P("fsdp", None),
    )
    return jax.shard_map(
        local, mesh=mesh, in_specs=placed, out_specs=P("img", "fsdp"), check_vma=False
    )
```

```python
import jax
import jax.numpy as jnp
from jax import lax
from jax.sharding import PartitionSpec as P

D = 8192
HEAD = 128
RHD = 96
PAIR = 2


eps_norm = 1e-05
eps_rms = 1e-06


def layer_norm(values, gain_vec):
    values = values.astype(jnp.float32)
    row_mean = jnp.mean(values, -1, keepdims=True)
    spread = jnp.mean(values * values, -1, keepdims=True) - row_mean * row_mean
    return (values - row_mean) * lax.rsqrt(spread + eps_norm) * gain_vec


def route_tables(wanted_images, per_owner, pair_slots):
    owners = wanted_images // per_owner
    slot_total = wanted_images.shape[1]
    positions = jnp.arange(slot_total, dtype=jnp.int32)
    before = (owners[:, :, None] == owners[:, None, :]) & (
        positions[None, None, :] < positions[None, :, None]
    )
    slot_rank = jnp.sum(before.astype(jnp.int32), axis=2)
    rank_hot = (
        slot_rank[:, :, None] == jnp.arange(pair_slots, dtype=jnp.int32)[None, None, :]
    ).astype(jnp.float32)
    return (owners, rank_hot)


def pack_rows(row_data, wanted_images, my_shard, per_owner, pair_slots):
    owners, rank_hot = route_tables(wanted_images, per_owner, pair_slots)
    is_mine = (owners == my_shard).astype(jnp.float32)
    local_hot = (
        (wanted_images % per_owner)[:, :, None]
        == jnp.arange(per_owner, dtype=jnp.int32)[None, None, :]
    ).astype(jnp.float32)
    picker = jnp.einsum("scp,sci->spi", rank_hot * is_mine[:, :, None], local_hot).astype(
        jnp.bfloat16
    )
    return jnp.einsum("spi,if->spf", picker, row_data, preferred_element_type=jnp.float32).astype(
        jnp.bfloat16
    )


def unpack_rows(received, wanted_images, my_shard, per_owner, pair_slots):
    owners, rank_hot = route_tables(wanted_images, per_owner, pair_slots)
    owner_row = lax.dynamic_slice_in_dim(owners, my_shard, 1, 0)[0]
    rank_row = lax.dynamic_slice_in_dim(rank_hot, my_shard, 1, 0)[0]
    source_hot = (
        owner_row[:, None] == jnp.arange(received.shape[0], dtype=jnp.int32)[None, :]
    ).astype(jnp.float32)
    taker = (source_hot[:, :, None] * rank_row[:, None, :]).astype(jnp.bfloat16)
    return jnp.einsum("cop,opf->cf", taker, received, preferred_element_type=jnp.float32).astype(
        jnp.bfloat16
    )


def gather_blocks(block, axis_name, parts):
    spread = jnp.broadcast_to(block[None], (parts,) + block.shape)
    return lax.all_to_all(spread, axis_name, split_axis=0, concat_axis=0, tiled=True)


def block_dot(rows, cols):
    contracted = jnp.einsum("brk,bkc->brc", rows, cols, preferred_element_type=jnp.float32)
    rounded = lax.reduce_precision(contracted, exponent_bits=8, mantissa_bits=7)
    return jnp.sum(rounded, 0)


def local(
    text_states,
    text_gain,
    gate_scale,
    live_counts,
    token_slot,
    wanted_images,
    patches,
    latent_init,
    context_gain,
    latent_gain,
    res_query,
    res_key,
    res_value,
    res_out,
    final_gain,
    cross_query,
    cross_key,
    cross_value,
    cross_out,
):
    my_feature = lax.axis_index("fsdp")
    my_shard = lax.axis_index("img")
    parts = lax.axis_size("fsdp")
    image_count = patches.shape[0]
    patch_count = patches.shape[1]
    feat_vis = patches.shape[2]
    latent_count = latent_init.shape[0]
    vis_width = latent_init.shape[1]
    res_cols = res_query.shape[1]
    res_heads = res_cols // RHD
    head_cols = cross_out.shape[0]
    token_count = text_states.shape[0]
    slot_count = wanted_images.shape[1]
    cross_heads = head_cols // HEAD
    contract_first = (((0,), (1,)), ((), ()))
    kv_weights = jnp.stack([cross_key, cross_value], 0).reshape(2, feat_vis, parts, head_cols)
    kv_weights = lax.all_to_all(
        jnp.transpose(kv_weights, (2, 0, 1, 3)), "fsdp", split_axis=0, concat_axis=0, tiled=True
    )
    text_f = text_states.astype(jnp.float32)
    gained = (text_f * text_gain).astype(jnp.bfloat16)
    after_weights = kv_weights[0, 0, 0, 0].astype(jnp.float32) * 0.0
    stats = jnp.concatenate([jnp.sum(text_f * text_f, -1), final_gain], 0) + after_weights
    stats = gather_blocks(stats, "fsdp", parts)
    squares = jnp.sum(stats[:, :token_count], 0)
    full_gain = stats[:, token_count:].reshape(vis_width)
    query_cols = lax.psum_scatter(
        lax.dot_general(
            cross_query, gained, contract_first, preferred_element_type=jnp.float32
        ).astype(jnp.bfloat16),
        "fsdp",
        scatter_dimension=0,
        tiled=True,
    )
    full_patches = lax.all_gather(patches, "fsdp", axis=2, tiled=True)
    context = layer_norm(full_patches, context_gain).astype(jnp.bfloat16)
    latent_normed = layer_norm(latent_init, latent_gain).astype(jnp.bfloat16)
    res_q_rows = jnp.dot(latent_normed, res_query, preferred_element_type=jnp.float32).astype(
        jnp.bfloat16
    )
    res_q_rows = res_q_rows.reshape(latent_count, res_heads, RHD)
    ctx_keys = jnp.einsum(
        "npv,vk->npk", context, res_key, preferred_element_type=jnp.float32
    ).astype(jnp.bfloat16)
    ctx_values = jnp.einsum(
        "npv,vk->npk", context, res_value, preferred_element_type=jnp.float32
    ).astype(jnp.bfloat16)
    lat_keys = jnp.dot(latent_normed, res_key, preferred_element_type=jnp.float32).astype(
        jnp.bfloat16
    )
    lat_values = jnp.dot(latent_normed, res_value, preferred_element_type=jnp.float32).astype(
        jnp.bfloat16
    )
    joined_shape = (image_count, latent_count, res_cols)
    key_rows = jnp.concatenate([ctx_keys, jnp.broadcast_to(lat_keys[None], joined_shape)], 1)
    value_rows = jnp.concatenate([ctx_values, jnp.broadcast_to(lat_values[None], joined_shape)], 1)
    key_rows = key_rows.reshape(image_count, patch_count + latent_count, res_heads, RHD)
    value_rows = value_rows.reshape(image_count, patch_count + latent_count, res_heads, RHD)
    res_scores = jnp.einsum(
        "rhe,nkhe->nhrk", res_q_rows, key_rows, preferred_element_type=jnp.float32
    ) * RHD ** (-0.5)
    res_weights = jnp.exp(res_scores)
    res_weights = (res_weights / jnp.sum(res_weights, -1, keepdims=True)).astype(jnp.bfloat16)
    res_mixed = jnp.einsum(
        "nhrk,nkhe->nrhe", res_weights, value_rows, preferred_element_type=jnp.float32
    )
    res_mixed = res_mixed.astype(jnp.bfloat16).reshape(image_count * latent_count, res_cols)
    row_total = image_count * latent_count
    row_part = row_total // parts
    head_part = jnp.dot(res_mixed, res_out, preferred_element_type=jnp.float32).astype(jnp.bfloat16)
    head_part = lax.all_to_all(
        head_part.reshape(parts, row_part, vis_width), "fsdp", split_axis=0, concat_axis=0, tiled=True
    )
    my_rows = my_feature * row_part
    init_rows = lax.dynamic_slice_in_dim(latent_init, my_rows % latent_count, row_part, 0)
    latents = init_rows.astype(jnp.float32) + jnp.sum(head_part.astype(jnp.float32), 0)
    resampled_rows = layer_norm(latents, full_gain).astype(jnp.bfloat16)
    resampled = lax.all_to_all(
        jnp.transpose(resampled_rows.reshape(row_part, parts, feat_vis), (1, 0, 2)),
        "fsdp",
        split_axis=0,
        concat_axis=0,
        tiled=True,
    )
    per_image = resampled.reshape(image_count, latent_count * feat_vis)
    outgoing = pack_rows(per_image, wanted_images, my_shard, image_count, PAIR)
    incoming = lax.all_to_all(outgoing, "img", split_axis=0, concat_axis=0, tiled=True)
    slot_latents = unpack_rows(incoming, wanted_images, my_shard, image_count, PAIR).reshape(
        slot_count * latent_count, feat_vis
    )
    slot_blocks = gather_blocks(slot_latents, "fsdp", parts)
    slot_keys = block_dot(slot_blocks, kv_weights[:, 0]).astype(jnp.bfloat16)
    slot_values = block_dot(slot_blocks, kv_weights[:, 1]).astype(jnp.bfloat16)
    slot_keys = slot_keys.reshape(slot_count, latent_count, cross_heads, HEAD)
    slot_values = slot_values.reshape(slot_count, latent_count, cross_heads, HEAD)
    token_scale = lax.rsqrt(squares / D + eps_rms)
    query_cols = (query_cols.astype(jnp.float32) * token_scale[None, :]).astype(jnp.bfloat16)
    query_heads = query_cols.reshape(cross_heads, HEAD, token_count)
    scores = jnp.einsum(
        "het,crhe->htcr", query_heads, slot_keys, preferred_element_type=jnp.float32
    ) * HEAD ** (-0.5)
    slot_hot = (token_slot[0][:, None] == jnp.arange(slot_count, dtype=jnp.int32)[None, :]).astype(
        jnp.float32
    )
    weights = jnp.exp(scores) * slot_hot[None, :, :, None]
    weights = (weights / jnp.sum(weights, axis=(2, 3), keepdims=True)).astype(jnp.bfloat16)
    attended = jnp.einsum(
        "htcr,crhe->het", weights, slot_values, preferred_element_type=jnp.float32
    )
    attended = attended.astype(jnp.bfloat16).reshape(head_cols, token_count)
    projected_cols = lax.psum_scatter(
        lax.dot_general(
            cross_out, attended, (((0,), (0,)), ((), ())), preferred_element_type=jnp.float32
        ).astype(jnp.bfloat16),
        "fsdp",
        scatter_dimension=0,
        tiled=True,
    ).astype(jnp.float32)
    projected = jnp.transpose(projected_cols)
    positions = jnp.arange(token_count, dtype=jnp.int32)
    live_mask = (positions < live_counts[0]).astype(jnp.float32)[:, None]
    return text_f + jnp.tanh(gate_scale) * projected * live_mask


def solution(mesh):
    placed = (
        P("img", "fsdp"),
        P("fsdp"),
        P("fsdp"),
        P("img"),
        P("img", None),
        P(),
        P("img", None, "fsdp"),
        P(),
        P(),
        P(),
        P(None, "fsdp"),
        P(None, "fsdp"),
        P(None, "fsdp"),
        P("fsdp", None),
        P("fsdp"),
        P("fsdp", None),
        P("fsdp", None),
        P("fsdp", None),
        P("fsdp", None),
    )
    return jax.shard_map(
        local, mesh=mesh, in_specs=placed, out_specs=P("img", "fsdp"), check_vma=False
    )
```

```python
import jax
import jax.numpy as jnp
from jax import lax
from jax.sharding import PartitionSpec as P

D = 8192
HEAD = 128
RHD = 96
PAIR = 2


eps_norm = 1e-05
eps_rms = 1e-06


def layer_norm(values, gain_vec):
    values = values.astype(jnp.float32)
    row_mean = jnp.mean(values, -1, keepdims=True)
    spread = jnp.mean(values * values, -1, keepdims=True) - row_mean * row_mean
    return (values - row_mean) * lax.rsqrt(spread + eps_norm) * gain_vec


def route_tables(wanted_images, per_owner, pair_slots):
    owners = wanted_images // per_owner
    slot_total = wanted_images.shape[1]
    positions = jnp.arange(slot_total, dtype=jnp.int32)
    before = (owners[:, :, None] == owners[:, None, :]) & (
        positions[None, None, :] < positions[None, :, None]
    )
    slot_rank = jnp.sum(before.astype(jnp.int32), axis=2)
    rank_hot = (
        slot_rank[:, :, None] == jnp.arange(pair_slots, dtype=jnp.int32)[None, None, :]
    ).astype(jnp.float32)
    return (owners, rank_hot)


def pack_rows(row_data, wanted_images, my_shard, per_owner, pair_slots):
    owners, rank_hot = route_tables(wanted_images, per_owner, pair_slots)
    is_mine = (owners == my_shard).astype(jnp.float32)
    local_hot = (
        (wanted_images % per_owner)[:, :, None]
        == jnp.arange(per_owner, dtype=jnp.int32)[None, None, :]
    ).astype(jnp.float32)
    picker = jnp.einsum("scp,sci->spi", rank_hot * is_mine[:, :, None], local_hot).astype(
        jnp.bfloat16
    )
    return jnp.einsum("spi,if->spf", picker, row_data, preferred_element_type=jnp.float32).astype(
        jnp.bfloat16
    )


def unpack_rows(received, wanted_images, my_shard, per_owner, pair_slots):
    owners, rank_hot = route_tables(wanted_images, per_owner, pair_slots)
    owner_row = lax.dynamic_slice_in_dim(owners, my_shard, 1, 0)[0]
    rank_row = lax.dynamic_slice_in_dim(rank_hot, my_shard, 1, 0)[0]
    source_hot = (
        owner_row[:, None] == jnp.arange(received.shape[0], dtype=jnp.int32)[None, :]
    ).astype(jnp.float32)
    taker = (source_hot[:, :, None] * rank_row[:, None, :]).astype(jnp.bfloat16)
    return jnp.einsum("cop,opf->cf", taker, received, preferred_element_type=jnp.float32).astype(
        jnp.bfloat16
    )


def gather_blocks(block, axis_name, parts):
    spread = jnp.broadcast_to(block[None], (parts,) + block.shape)
    return lax.all_to_all(spread, axis_name, split_axis=0, concat_axis=0, tiled=True)


def block_dot(rows, cols):
    contracted = jnp.einsum("brk,bkc->brc", rows, cols, preferred_element_type=jnp.float32)
    rounded = lax.reduce_precision(contracted, exponent_bits=8, mantissa_bits=7)
    return jnp.sum(rounded, 0)


def local(
    text_states,
    text_gain,
    gate_scale,
    live_counts,
    token_slot,
    wanted_images,
    patches,
    latent_init,
    context_gain,
    latent_gain,
    res_query,
    res_key,
    res_value,
    res_out,
    final_gain,
    cross_query,
    cross_key,
    cross_value,
    cross_out,
):
    my_feature = lax.axis_index("fsdp")
    my_shard = lax.axis_index("img")
    parts = lax.axis_size("fsdp")
    image_count = patches.shape[0]
    patch_count = patches.shape[1]
    feat_vis = patches.shape[2]
    latent_count = latent_init.shape[0]
    vis_width = latent_init.shape[1]
    res_cols = res_query.shape[1]
    res_heads = res_cols // RHD
    head_cols = cross_out.shape[0]
    token_count = text_states.shape[0]
    slot_count = wanted_images.shape[1]
    cross_heads = head_cols // HEAD
    contract_first = (((0,), (1,)), ((), ()))
    kv_weights = jnp.stack([cross_key, cross_value], 1).reshape(feat_vis, 2, parts, head_cols)
    kv_weights = lax.all_to_all(
        jnp.transpose(kv_weights, (2, 0, 1, 3)), "fsdp", split_axis=0, concat_axis=0, tiled=True
    ).reshape(parts, feat_vis, 2 * head_cols)
    text_f = text_states.astype(jnp.float32)
    gained = (text_f * text_gain).astype(jnp.bfloat16)
    after_weights = kv_weights[0, 0, 0].astype(jnp.float32) * 0.0
    stats = jnp.concatenate([jnp.sum(text_f * text_f, -1), final_gain], 0) + after_weights
    stats = gather_blocks(stats, "fsdp", parts)
    squares = jnp.sum(stats[:, :token_count], 0)
    full_gain = stats[:, token_count:].reshape(vis_width)
    query_cols = lax.psum_scatter(
        lax.dot_general(
            cross_query, gained, contract_first, preferred_element_type=jnp.float32
        ).astype(jnp.bfloat16),
        "fsdp",
        scatter_dimension=0,
        tiled=True,
    )
    full_patches = lax.all_gather(patches, "fsdp", axis=2, tiled=True)
    context = layer_norm(full_patches, context_gain).astype(jnp.bfloat16)
    latent_normed = layer_norm(latent_init, latent_gain).astype(jnp.bfloat16)
    res_q_rows = jnp.dot(latent_normed, res_query, preferred_element_type=jnp.float32).astype(
        jnp.bfloat16
    )
    res_q_rows = res_q_rows.reshape(latent_count, res_heads, RHD)
    ctx_keys = jnp.einsum(
        "npv,vk->npk", context, res_key, preferred_element_type=jnp.float32
    ).astype(jnp.bfloat16)
    ctx_values = jnp.einsum(
        "npv,vk->npk", context, res_value, preferred_element_type=jnp.float32
    ).astype(jnp.bfloat16)
    lat_keys = jnp.dot(latent_normed, res_key, preferred_element_type=jnp.float32).astype(
        jnp.bfloat16
    )
    lat_values = jnp.dot(latent_normed, res_value, preferred_element_type=jnp.float32).astype(
        jnp.bfloat16
    )
    joined_shape = (image_count, latent_count, res_cols)
    key_rows = jnp.concatenate([ctx_keys, jnp.broadcast_to(lat_keys[None], joined_shape)], 1)
    value_rows = jnp.concatenate([ctx_values, jnp.broadcast_to(lat_values[None], joined_shape)], 1)
    key_rows = key_rows.reshape(image_count, patch_count + latent_count, res_heads, RHD)
    value_rows = value_rows.reshape(image_count, patch_count + latent_count, res_heads, RHD)
    res_scores = jnp.einsum(
        "rhe,nkhe->nhrk", res_q_rows, key_rows, preferred_element_type=jnp.float32
    ) * RHD ** (-0.5)
    res_weights = jnp.exp(res_scores)
    res_weights = (res_weights / jnp.sum(res_weights, -1, keepdims=True)).astype(jnp.bfloat16)
    res_mixed = jnp.einsum(
        "nhrk,nkhe->nrhe", res_weights, value_rows, preferred_element_type=jnp.float32
    )
    res_mixed = res_mixed.astype(jnp.bfloat16).reshape(image_count * latent_count, res_cols)
    row_total = image_count * latent_count
    row_part = row_total // parts
    head_part = jnp.dot(res_mixed, res_out, preferred_element_type=jnp.float32).astype(jnp.bfloat16)
    head_part = lax.all_to_all(
        head_part.reshape(parts, row_part, vis_width), "fsdp", split_axis=0, concat_axis=0, tiled=True
    )
    my_rows = my_feature * row_part
    init_rows = lax.dynamic_slice_in_dim(latent_init, my_rows % latent_count, row_part, 0)
    latents = init_rows.astype(jnp.float32) + jnp.sum(head_part.astype(jnp.float32), 0)
    resampled_rows = layer_norm(latents, full_gain).astype(jnp.bfloat16)
    resampled = lax.all_to_all(
        jnp.transpose(resampled_rows.reshape(row_part, parts, feat_vis), (1, 0, 2)),
        "fsdp",
        split_axis=0,
        concat_axis=0,
        tiled=True,
    )
    per_image = resampled.reshape(image_count, latent_count * feat_vis)
    outgoing = pack_rows(per_image, wanted_images, my_shard, image_count, PAIR)
    incoming = lax.all_to_all(outgoing, "img", split_axis=0, concat_axis=0, tiled=True)
    slot_latents = unpack_rows(incoming, wanted_images, my_shard, image_count, PAIR).reshape(
        slot_count * latent_count, feat_vis
    )
    slot_blocks = gather_blocks(slot_latents, "fsdp", parts)
    slot_kv = block_dot(slot_blocks, kv_weights).astype(jnp.bfloat16)
    slot_kv = slot_kv.reshape(slot_count, latent_count, 2, cross_heads, HEAD)
    slot_keys = slot_kv[:, :, 0]
    slot_values = slot_kv[:, :, 1]
    token_scale = lax.rsqrt(squares / D + eps_rms)
    query_cols = (query_cols.astype(jnp.float32) * token_scale[None, :]).astype(jnp.bfloat16)
    query_heads = query_cols.reshape(cross_heads, HEAD, token_count)
    scores = jnp.einsum(
        "het,crhe->htcr", query_heads, slot_keys, preferred_element_type=jnp.float32
    ) * HEAD ** (-0.5)
    slot_hot = (token_slot[0][:, None] == jnp.arange(slot_count, dtype=jnp.int32)[None, :]).astype(
        jnp.float32
    )
    weights = jnp.exp(scores) * slot_hot[None, :, :, None]
    weights = (weights / jnp.sum(weights, axis=(2, 3), keepdims=True)).astype(jnp.bfloat16)
    attended = jnp.einsum(
        "htcr,crhe->het", weights, slot_values, preferred_element_type=jnp.float32
    )
    attended = attended.astype(jnp.bfloat16).reshape(head_cols, token_count)
    projected_cols = lax.psum_scatter(
        lax.dot_general(
            cross_out, attended, (((0,), (0,)), ((), ())), preferred_element_type=jnp.float32
        ).astype(jnp.bfloat16),
        "fsdp",
        scatter_dimension=0,
        tiled=True,
    ).astype(jnp.float32)
    projected = jnp.transpose(projected_cols)
    positions = jnp.arange(token_count, dtype=jnp.int32)
    live_mask = (positions < live_counts[0]).astype(jnp.float32)[:, None]
    return text_f + jnp.tanh(gate_scale) * projected * live_mask


def solution(mesh):
    placed = (
        P("img", "fsdp"),
        P("fsdp"),
        P("fsdp"),
        P("img"),
        P("img", None),
        P(),
        P("img", None, "fsdp"),
        P(),
        P(),
        P(),
        P(None, "fsdp"),
        P(None, "fsdp"),
        P(None, "fsdp"),
        P("fsdp", None),
        P("fsdp"),
        P("fsdp", None),
        P("fsdp", None),
        P("fsdp", None),
        P("fsdp", None),
    )
    return jax.shard_map(
        local, mesh=mesh, in_specs=placed, out_specs=P("img", "fsdp"), check_vma=False
    )
```

```python
import jax
import jax.numpy as jnp
from jax import lax
from jax.sharding import PartitionSpec as P

D = 8192
HEAD = 128
RHD = 96
PAIR = 2


eps_norm = 1e-05
eps_rms = 1e-06


def layer_norm(values, gain_vec):
    values = values.astype(jnp.float32)
    row_mean = jnp.mean(values, -1, keepdims=True)
    spread = jnp.mean(values * values, -1, keepdims=True) - row_mean * row_mean
    return (values - row_mean) * lax.rsqrt(spread + eps_norm) * gain_vec


def route_tables(wanted_images, per_owner, pair_slots):
    owners = wanted_images // per_owner
    slot_total = wanted_images.shape[1]
    positions = jnp.arange(slot_total, dtype=jnp.int32)
    before = (owners[:, :, None] == owners[:, None, :]) & (
        positions[None, None, :] < positions[None, :, None]
    )
    slot_rank = jnp.sum(before.astype(jnp.int32), axis=2)
    rank_hot = (
        slot_rank[:, :, None] == jnp.arange(pair_slots, dtype=jnp.int32)[None, None, :]
    ).astype(jnp.float32)
    return (owners, rank_hot)


def pack_rows(row_data, wanted_images, my_shard, per_owner, pair_slots):
    owners, rank_hot = route_tables(wanted_images, per_owner, pair_slots)
    is_mine = (owners == my_shard).astype(jnp.float32)
    local_hot = (
        (wanted_images % per_owner)[:, :, None]
        == jnp.arange(per_owner, dtype=jnp.int32)[None, None, :]
    ).astype(jnp.float32)
    picker = jnp.einsum("scp,sci->spi", rank_hot * is_mine[:, :, None], local_hot).astype(
        jnp.bfloat16
    )
    return jnp.einsum("spi,if->spf", picker, row_data, preferred_element_type=jnp.float32).astype(
        jnp.bfloat16
    )


def unpack_rows(received, wanted_images, my_shard, per_owner, pair_slots):
    owners, rank_hot = route_tables(wanted_images, per_owner, pair_slots)
    owner_row = lax.dynamic_slice_in_dim(owners, my_shard, 1, 0)[0]
    rank_row = lax.dynamic_slice_in_dim(rank_hot, my_shard, 1, 0)[0]
    source_hot = (
        owner_row[:, None] == jnp.arange(received.shape[0], dtype=jnp.int32)[None, :]
    ).astype(jnp.float32)
    taker = (source_hot[:, :, None] * rank_row[:, None, :]).astype(jnp.bfloat16)
    return jnp.einsum("cop,opf->cf", taker, received, preferred_element_type=jnp.float32).astype(
        jnp.bfloat16
    )


def gather_blocks(block, axis_name, parts):
    spread = jnp.broadcast_to(block[None], (parts,) + block.shape)
    return lax.all_to_all(spread, axis_name, split_axis=0, concat_axis=0, tiled=True)


def block_dot(rows, cols):
    contracted = jnp.einsum("brk,bkc->brc", rows, cols, preferred_element_type=jnp.float32)
    rounded = lax.reduce_precision(contracted, exponent_bits=8, mantissa_bits=7)
    return jnp.sum(rounded, 0)


def local(
    text_states,
    text_gain,
    gate_scale,
    live_counts,
    token_slot,
    wanted_images,
    patches,
    latent_init,
    context_gain,
    latent_gain,
    res_query,
    res_key,
    res_value,
    res_out,
    final_gain,
    cross_query,
    cross_key,
    cross_value,
    cross_out,
):
    my_feature = lax.axis_index("fsdp")
    my_shard = lax.axis_index("img")
    parts = lax.axis_size("fsdp")
    image_count = patches.shape[0]
    patch_count = patches.shape[1]
    feat_vis = patches.shape[2]
    latent_count = latent_init.shape[0]
    vis_width = latent_init.shape[1]
    res_cols = res_query.shape[1]
    res_heads = res_cols // RHD
    head_cols = cross_out.shape[0]
    token_count = text_states.shape[0]
    slot_count = wanted_images.shape[1]
    cross_heads = head_cols // HEAD
    contract_first = (((0,), (1,)), ((), ()))
    kv_weights = jnp.stack([cross_key, cross_value], 0).reshape(2, feat_vis, parts, head_cols)
    kv_weights = lax.all_to_all(
        jnp.transpose(kv_weights, (2, 0, 1, 3)), "fsdp", split_axis=0, concat_axis=0, tiled=True
    )
    text_f = text_states.astype(jnp.float32)
    gained = (text_f * text_gain).astype(jnp.bfloat16)
    after_weights = kv_weights[0, 0, 0, 0].astype(jnp.float32) * 0.0
    stats = jnp.concatenate([jnp.sum(text_f * text_f, -1), final_gain], 0) + after_weights
    stats = gather_blocks(stats, "fsdp", parts)
    squares = jnp.sum(stats[:, :token_count], 0)
    full_gain = stats[:, token_count:].reshape(vis_width)
    query_cols = lax.psum_scatter(
        lax.dot_general(
            cross_query, gained, contract_first, preferred_element_type=jnp.float32
        ).astype(jnp.bfloat16),
        "fsdp",
        scatter_dimension=0,
        tiled=True,
    )
    full_patches = lax.all_gather(patches, "fsdp", axis=2, tiled=True)
    context = layer_norm(full_patches, context_gain).astype(jnp.bfloat16)
    latent_normed = layer_norm(latent_init, latent_gain).astype(jnp.bfloat16)
    res_q_rows = jnp.dot(latent_normed, res_query, preferred_element_type=jnp.float32).astype(
        jnp.bfloat16
    )
    res_q_rows = res_q_rows.reshape(latent_count, res_heads, RHD)
    ctx_keys = jnp.einsum(
        "npv,vk->npk", context, res_key, preferred_element_type=jnp.float32
    ).astype(jnp.bfloat16)
    ctx_values = jnp.einsum(
        "npv,vk->npk", context, res_value, preferred_element_type=jnp.float32
    ).astype(jnp.bfloat16)
    lat_keys = jnp.dot(latent_normed, res_key, preferred_element_type=jnp.float32).astype(
        jnp.bfloat16
    )
    lat_values = jnp.dot(latent_normed, res_value, preferred_element_type=jnp.float32).astype(
        jnp.bfloat16
    )
    joined_shape = (image_count, latent_count, res_cols)
    key_rows = jnp.concatenate([ctx_keys, jnp.broadcast_to(lat_keys[None], joined_shape)], 1)
    value_rows = jnp.concatenate([ctx_values, jnp.broadcast_to(lat_values[None], joined_shape)], 1)
    key_rows = key_rows.reshape(image_count, patch_count + latent_count, res_heads, RHD)
    value_rows = value_rows.reshape(image_count, patch_count + latent_count, res_heads, RHD)
    res_scores = jnp.einsum(
        "rhe,nkhe->nhrk", res_q_rows, key_rows, preferred_element_type=jnp.float32
    ) * RHD ** (-0.5)
    res_weights = jnp.exp(res_scores)
    res_weights = (res_weights / jnp.sum(res_weights, -1, keepdims=True)).astype(jnp.bfloat16)
    res_mixed = jnp.einsum(
        "nhrk,nkhe->nrhe", res_weights, value_rows, preferred_element_type=jnp.float32
    )
    res_mixed = res_mixed.astype(jnp.bfloat16).reshape(image_count * latent_count, res_cols)
    row_total = image_count * latent_count
    row_part = row_total // parts
    head_part = jnp.dot(res_mixed, res_out, preferred_element_type=jnp.float32).astype(jnp.bfloat16)
    head_part = lax.all_to_all(
        head_part.reshape(parts, row_part, vis_width), "fsdp", split_axis=0, concat_axis=0, tiled=True
    )
    my_rows = my_feature * row_part
    init_rows = lax.dynamic_slice_in_dim(latent_init, my_rows % latent_count, row_part, 0)
    latents = init_rows.astype(jnp.float32) + jnp.sum(head_part.astype(jnp.float32), 0)
    resampled_rows = layer_norm(latents, full_gain).astype(jnp.bfloat16)
    resampled = lax.all_to_all(
        jnp.transpose(resampled_rows.reshape(row_part, parts, feat_vis), (1, 0, 2)),
        "fsdp",
        split_axis=0,
        concat_axis=0,
        tiled=True,
    )
    per_image = resampled.reshape(image_count, latent_count * feat_vis)
    outgoing = pack_rows(per_image, wanted_images, my_shard, image_count, PAIR)
    incoming = lax.all_to_all(outgoing, "img", split_axis=0, concat_axis=0, tiled=True)
    slot_latents = unpack_rows(incoming, wanted_images, my_shard, image_count, PAIR).reshape(
        slot_count * latent_count, feat_vis
    )
    slot_blocks = gather_blocks(slot_latents, "fsdp", parts)
    slot_kv = jnp.einsum("brk,bskc->brsc", slot_blocks, kv_weights, preferred_element_type=jnp.float32)
    slot_kv = jnp.sum(lax.reduce_precision(slot_kv, exponent_bits=8, mantissa_bits=7), 0)
    slot_kv = slot_kv.astype(jnp.bfloat16).reshape(slot_count, latent_count, 2, cross_heads, HEAD)
    slot_keys = slot_kv[:, :, 0]
    slot_values = slot_kv[:, :, 1]
    token_scale = lax.rsqrt(squares / D + eps_rms)
    query_cols = (query_cols.astype(jnp.float32) * token_scale[None, :]).astype(jnp.bfloat16)
    query_heads = query_cols.reshape(cross_heads, HEAD, token_count)
    scores = jnp.einsum(
        "het,crhe->htcr", query_heads, slot_keys, preferred_element_type=jnp.float32
    ) * HEAD ** (-0.5)
    slot_hot = (token_slot[0][:, None] == jnp.arange(slot_count, dtype=jnp.int32)[None, :]).astype(
        jnp.float32
    )
    weights = jnp.exp(scores) * slot_hot[None, :, :, None]
    weights = (weights / jnp.sum(weights, axis=(2, 3), keepdims=True)).astype(jnp.bfloat16)
    attended = jnp.einsum(
        "htcr,crhe->het", weights, slot_values, preferred_element_type=jnp.float32
    )
    attended = attended.astype(jnp.bfloat16).reshape(head_cols, token_count)
    projected_cols = lax.psum_scatter(
        lax.dot_general(
            cross_out, attended, (((0,), (0,)), ((), ())), preferred_element_type=jnp.float32
        ).astype(jnp.bfloat16),
        "fsdp",
        scatter_dimension=0,
        tiled=True,
    ).astype(jnp.float32)
    projected = jnp.transpose(projected_cols)
    positions = jnp.arange(token_count, dtype=jnp.int32)
    live_mask = (positions < live_counts[0]).astype(jnp.float32)[:, None]
    return text_f + jnp.tanh(gate_scale) * projected * live_mask


def solution(mesh):
    placed = (
        P("img", "fsdp"),
        P("fsdp"),
        P("fsdp"),
        P("img"),
        P("img", None),
        P(),
        P("img", None, "fsdp"),
        P(),
        P(),
        P(),
        P(None, "fsdp"),
        P(None, "fsdp"),
        P(None, "fsdp"),
        P("fsdp", None),
        P("fsdp"),
        P("fsdp", None),
        P("fsdp", None),
        P("fsdp", None),
        P("fsdp", None),
    )
    return jax.shard_map(
        local, mesh=mesh, in_specs=placed, out_specs=P("img", "fsdp"), check_vma=False
    )
```

```python
import jax
import jax.numpy as jnp
from jax import lax
from jax.sharding import PartitionSpec as P

D = 8192
HEAD = 128
RHD = 96
PAIR = 2


eps_norm = 1e-05
eps_rms = 1e-06


def layer_norm(values, gain_vec):
    values = values.astype(jnp.float32)
    row_mean = jnp.mean(values, -1, keepdims=True)
    spread = jnp.mean(values * values, -1, keepdims=True) - row_mean * row_mean
    return (values - row_mean) * lax.rsqrt(spread + eps_norm) * gain_vec


def route_tables(wanted_images, per_owner, pair_slots):
    owners = wanted_images // per_owner
    slot_total = wanted_images.shape[1]
    positions = jnp.arange(slot_total, dtype=jnp.int32)
    before = (owners[:, :, None] == owners[:, None, :]) & (
        positions[None, None, :] < positions[None, :, None]
    )
    slot_rank = jnp.sum(before.astype(jnp.int32), axis=2)
    rank_hot = (
        slot_rank[:, :, None] == jnp.arange(pair_slots, dtype=jnp.int32)[None, None, :]
    ).astype(jnp.float32)
    return (owners, rank_hot)


def pack_rows(row_data, wanted_images, my_shard, per_owner, pair_slots):
    owners, rank_hot = route_tables(wanted_images, per_owner, pair_slots)
    is_mine = (owners == my_shard).astype(jnp.float32)
    local_hot = (
        (wanted_images % per_owner)[:, :, None]
        == jnp.arange(per_owner, dtype=jnp.int32)[None, None, :]
    ).astype(jnp.float32)
    picker = jnp.einsum("scp,sci->spi", rank_hot * is_mine[:, :, None], local_hot).astype(
        jnp.bfloat16
    )
    return jnp.einsum("spi,if->spf", picker, row_data, preferred_element_type=jnp.float32).astype(
        jnp.bfloat16
    )


def unpack_rows(received, wanted_images, my_shard, per_owner, pair_slots):
    owners, rank_hot = route_tables(wanted_images, per_owner, pair_slots)
    owner_row = lax.dynamic_slice_in_dim(owners, my_shard, 1, 0)[0]
    rank_row = lax.dynamic_slice_in_dim(rank_hot, my_shard, 1, 0)[0]
    source_hot = (
        owner_row[:, None] == jnp.arange(received.shape[0], dtype=jnp.int32)[None, :]
    ).astype(jnp.float32)
    taker = (source_hot[:, :, None] * rank_row[:, None, :]).astype(jnp.bfloat16)
    return jnp.einsum("cop,opf->cf", taker, received, preferred_element_type=jnp.float32).astype(
        jnp.bfloat16
    )


def gather_blocks(block, axis_name, parts):
    spread = jnp.broadcast_to(block[None], (parts,) + block.shape)
    return lax.all_to_all(spread, axis_name, split_axis=0, concat_axis=0, tiled=True)


def block_dot(rows, cols):
    contracted = jnp.einsum("brk,bkc->brc", rows, cols, preferred_element_type=jnp.float32)
    rounded = lax.reduce_precision(contracted, exponent_bits=8, mantissa_bits=7)
    return jnp.sum(rounded, 0)


def local(
    text_states,
    text_gain,
    gate_scale,
    live_counts,
    token_slot,
    wanted_images,
    patches,
    latent_init,
    context_gain,
    latent_gain,
    res_query,
    res_key,
    res_value,
    res_out,
    final_gain,
    cross_query,
    cross_key,
    cross_value,
    cross_out,
):
    my_feature = lax.axis_index("fsdp")
    my_shard = lax.axis_index("img")
    parts = lax.axis_size("fsdp")
    image_count = patches.shape[0]
    patch_count = patches.shape[1]
    feat_vis = patches.shape[2]
    latent_count = latent_init.shape[0]
    vis_width = latent_init.shape[1]
    res_cols = res_query.shape[1]
    res_heads = res_cols // RHD
    head_cols = cross_out.shape[0]
    token_count = text_states.shape[0]
    slot_count = wanted_images.shape[1]
    cross_heads = head_cols // HEAD
    contract_first = (((0,), (1,)), ((), ()))
    my_core = my_shard % 2
    kv_stack = jnp.stack([cross_key, cross_value], 0)
    my_kind = lax.dynamic_index_in_dim(kv_stack, my_core, 0, keepdims=False)
    my_kind = jnp.transpose(my_kind.reshape(feat_vis, parts, head_cols), (1, 0, 2))
    my_kind = lax.all_to_all(my_kind, "fsdp", split_axis=0, concat_axis=0, tiled=True)
    core_pairs = [(j, j ^ 1) for j in range(lax.axis_size("img"))]
    other_kind = lax.ppermute(my_kind, "img", core_pairs)
    kv_weights = jnp.stack([my_kind, other_kind], 1)
    text_f = text_states.astype(jnp.float32)
    gained = (text_f * text_gain).astype(jnp.bfloat16)
    after_weights = my_kind[0, 0, 0].astype(jnp.float32) * 0.0
    stats = jnp.concatenate([jnp.sum(text_f * text_f, -1), final_gain], 0) + after_weights
    stats = gather_blocks(stats, "fsdp", parts)
    squares = jnp.sum(stats[:, :token_count], 0)
    full_gain = stats[:, token_count:].reshape(vis_width)
    query_cols = lax.psum_scatter(
        lax.dot_general(
            cross_query, gained, contract_first, preferred_element_type=jnp.float32
        ).astype(jnp.bfloat16),
        "fsdp",
        scatter_dimension=0,
        tiled=True,
    )
    full_patches = lax.all_gather(patches, "fsdp", axis=2, tiled=True)
    context = layer_norm(full_patches, context_gain).astype(jnp.bfloat16)
    latent_normed = layer_norm(latent_init, latent_gain).astype(jnp.bfloat16)
    res_q_rows = jnp.dot(latent_normed, res_query, preferred_element_type=jnp.float32).astype(
        jnp.bfloat16
    )
    res_q_rows = res_q_rows.reshape(latent_count, res_heads, RHD)
    ctx_keys = jnp.einsum(
        "npv,vk->npk", context, res_key, preferred_element_type=jnp.float32
    ).astype(jnp.bfloat16)
    ctx_values = jnp.einsum(
        "npv,vk->npk", context, res_value, preferred_element_type=jnp.float32
    ).astype(jnp.bfloat16)
    lat_keys = jnp.dot(latent_normed, res_key, preferred_element_type=jnp.float32).astype(
        jnp.bfloat16
    )
    lat_values = jnp.dot(latent_normed, res_value, preferred_element_type=jnp.float32).astype(
        jnp.bfloat16
    )
    joined_shape = (image_count, latent_count, res_cols)
    key_rows = jnp.concatenate([ctx_keys, jnp.broadcast_to(lat_keys[None], joined_shape)], 1)
    value_rows = jnp.concatenate([ctx_values, jnp.broadcast_to(lat_values[None], joined_shape)], 1)
    key_rows = key_rows.reshape(image_count, patch_count + latent_count, res_heads, RHD)
    value_rows = value_rows.reshape(image_count, patch_count + latent_count, res_heads, RHD)
    res_scores = jnp.einsum(
        "rhe,nkhe->nhrk", res_q_rows, key_rows, preferred_element_type=jnp.float32
    ) * RHD ** (-0.5)
    res_weights = jnp.exp(res_scores)
    res_weights = (res_weights / jnp.sum(res_weights, -1, keepdims=True)).astype(jnp.bfloat16)
    res_mixed = jnp.einsum(
        "nhrk,nkhe->nrhe", res_weights, value_rows, preferred_element_type=jnp.float32
    )
    res_mixed = res_mixed.astype(jnp.bfloat16).reshape(image_count * latent_count, res_cols)
    row_total = image_count * latent_count
    row_part = row_total // parts
    head_part = jnp.dot(res_mixed, res_out, preferred_element_type=jnp.float32).astype(jnp.bfloat16)
    head_part = lax.all_to_all(
        head_part.reshape(parts, row_part, vis_width), "fsdp", split_axis=0, concat_axis=0, tiled=True
    )
    my_rows = my_feature * row_part
    init_rows = lax.dynamic_slice_in_dim(latent_init, my_rows % latent_count, row_part, 0)
    latents = init_rows.astype(jnp.float32) + jnp.sum(head_part.astype(jnp.float32), 0)
    resampled_rows = layer_norm(latents, full_gain).astype(jnp.bfloat16)
    resampled = lax.all_to_all(
        jnp.transpose(resampled_rows.reshape(row_part, parts, feat_vis), (1, 0, 2)),
        "fsdp",
        split_axis=0,
        concat_axis=0,
        tiled=True,
    )
    per_image = resampled.reshape(image_count, latent_count * feat_vis)
    outgoing = pack_rows(per_image, wanted_images, my_shard, image_count, PAIR)
    incoming = lax.all_to_all(outgoing, "img", split_axis=0, concat_axis=0, tiled=True)
    slot_latents = unpack_rows(incoming, wanted_images, my_shard, image_count, PAIR).reshape(
        slot_count * latent_count, feat_vis
    )
    slot_blocks = gather_blocks(slot_latents, "fsdp", parts)
    slot_kv = jnp.einsum("brk,bskc->brsc", slot_blocks, kv_weights, preferred_element_type=jnp.float32)
    slot_kv = jnp.sum(lax.reduce_precision(slot_kv, exponent_bits=8, mantissa_bits=7), 0)
    slot_kv = slot_kv.astype(jnp.bfloat16).reshape(slot_count, latent_count, 2, cross_heads, HEAD)
    slot_keys = lax.dynamic_index_in_dim(slot_kv, my_core, 2, keepdims=False)
    slot_values = lax.dynamic_index_in_dim(slot_kv, 1 - my_core, 2, keepdims=False)
    token_scale = lax.rsqrt(squares / D + eps_rms)
    query_cols = (query_cols.astype(jnp.float32) * token_scale[None, :]).astype(jnp.bfloat16)
    query_heads = query_cols.reshape(cross_heads, HEAD, token_count)
    scores = jnp.einsum(
        "het,crhe->htcr", query_heads, slot_keys, preferred_element_type=jnp.float32
    ) * HEAD ** (-0.5)
    slot_hot = (token_slot[0][:, None] == jnp.arange(slot_count, dtype=jnp.int32)[None, :]).astype(
        jnp.float32
    )
    weights = jnp.exp(scores) * slot_hot[None, :, :, None]
    weights = (weights / jnp.sum(weights, axis=(2, 3), keepdims=True)).astype(jnp.bfloat16)
    attended = jnp.einsum(
        "htcr,crhe->het", weights, slot_values, preferred_element_type=jnp.float32
    )
    attended = attended.astype(jnp.bfloat16).reshape(head_cols, token_count)
    projected_cols = lax.psum_scatter(
        lax.dot_general(
            cross_out, attended, (((0,), (0,)), ((), ())), preferred_element_type=jnp.float32
        ).astype(jnp.bfloat16),
        "fsdp",
        scatter_dimension=0,
        tiled=True,
    ).astype(jnp.float32)
    projected = jnp.transpose(projected_cols)
    positions = jnp.arange(token_count, dtype=jnp.int32)
    live_mask = (positions < live_counts[0]).astype(jnp.float32)[:, None]
    return text_f + jnp.tanh(gate_scale) * projected * live_mask


def solution(mesh):
    placed = (
        P("img", "fsdp"),
        P("fsdp"),
        P("fsdp"),
        P("img"),
        P("img", None),
        P(),
        P("img", None, "fsdp"),
        P(),
        P(),
        P(),
        P(None, "fsdp"),
        P(None, "fsdp"),
        P(None, "fsdp"),
        P("fsdp", None),
        P("fsdp"),
        P("fsdp", None),
        P("fsdp", None),
        P("fsdp", None),
        P("fsdp", None),
    )
    return jax.shard_map(
        local, mesh=mesh, in_specs=placed, out_specs=P("img", "fsdp"), check_vma=False
    )
```

```python
import jax
import jax.numpy as jnp
from jax import lax
from jax.sharding import PartitionSpec as P

D = 8192
HEAD = 128
RHD = 96
PAIR = 2


eps_norm = 1e-05
eps_rms = 1e-06


def layer_norm(values, gain_vec):
    values = values.astype(jnp.float32)
    row_mean = jnp.mean(values, -1, keepdims=True)
    spread = jnp.mean(values * values, -1, keepdims=True) - row_mean * row_mean
    return (values - row_mean) * lax.rsqrt(spread + eps_norm) * gain_vec


def route_tables(wanted_images, per_owner, pair_slots):
    owners = wanted_images // per_owner
    slot_total = wanted_images.shape[1]
    positions = jnp.arange(slot_total, dtype=jnp.int32)
    before = (owners[:, :, None] == owners[:, None, :]) & (
        positions[None, None, :] < positions[None, :, None]
    )
    slot_rank = jnp.sum(before.astype(jnp.int32), axis=2)
    rank_hot = (
        slot_rank[:, :, None] == jnp.arange(pair_slots, dtype=jnp.int32)[None, None, :]
    ).astype(jnp.float32)
    return (owners, rank_hot)


def pack_rows(row_data, wanted_images, my_shard, per_owner, pair_slots):
    owners, rank_hot = route_tables(wanted_images, per_owner, pair_slots)
    is_mine = (owners == my_shard).astype(jnp.float32)
    local_hot = (
        (wanted_images % per_owner)[:, :, None]
        == jnp.arange(per_owner, dtype=jnp.int32)[None, None, :]
    ).astype(jnp.float32)
    picker = jnp.einsum("scp,sci->spi", rank_hot * is_mine[:, :, None], local_hot).astype(
        jnp.bfloat16
    )
    return jnp.einsum("spi,if->spf", picker, row_data, preferred_element_type=jnp.float32).astype(
        jnp.bfloat16
    )


def unpack_rows(received, wanted_images, my_shard, per_owner, pair_slots):
    owners, rank_hot = route_tables(wanted_images, per_owner, pair_slots)
    owner_row = lax.dynamic_slice_in_dim(owners, my_shard, 1, 0)[0]
    rank_row = lax.dynamic_slice_in_dim(rank_hot, my_shard, 1, 0)[0]
    source_hot = (
        owner_row[:, None] == jnp.arange(received.shape[0], dtype=jnp.int32)[None, :]
    ).astype(jnp.float32)
    taker = (source_hot[:, :, None] * rank_row[:, None, :]).astype(jnp.bfloat16)
    return jnp.einsum("cop,opf->cf", taker, received, preferred_element_type=jnp.float32).astype(
        jnp.bfloat16
    )


def gather_blocks(block, axis_name, parts):
    spread = jnp.broadcast_to(block[None], (parts,) + block.shape)
    return lax.all_to_all(spread, axis_name, split_axis=0, concat_axis=0, tiled=True)


def block_dot(rows, cols):
    contracted = jnp.einsum("brk,bkc->brc", rows, cols, preferred_element_type=jnp.float32)
    rounded = lax.reduce_precision(contracted, exponent_bits=8, mantissa_bits=7)
    return jnp.sum(rounded, 0)


def local(
    text_states,
    text_gain,
    gate_scale,
    live_counts,
    token_slot,
    wanted_images,
    patches,
    latent_init,
    context_gain,
    latent_gain,
    res_query,
    res_key,
    res_value,
    res_out,
    final_gain,
    cross_query,
    cross_key,
    cross_value,
    cross_out,
):
    my_feature = lax.axis_index("fsdp")
    my_shard = lax.axis_index("img")
    parts = lax.axis_size("fsdp")
    image_count = patches.shape[0]
    patch_count = patches.shape[1]
    feat_vis = patches.shape[2]
    latent_count = latent_init.shape[0]
    vis_width = latent_init.shape[1]
    res_cols = res_query.shape[1]
    res_heads = res_cols // RHD
    head_cols = cross_out.shape[0]
    token_count = text_states.shape[0]
    slot_count = wanted_images.shape[1]
    cross_heads = head_cols // HEAD
    contract_first = (((0,), (1,)), ((), ()))
    my_core = my_shard % 2
    kv_stack = jnp.stack([cross_key, cross_value], 0)
    patch_blocks = gather_blocks(patches, "fsdp", parts)
    after_patches = patch_blocks[0, 0, 0, 0] * 0
    my_kind = lax.dynamic_index_in_dim(kv_stack, my_core, 0, keepdims=False) + after_patches
    my_kind = jnp.transpose(my_kind.reshape(feat_vis, parts, head_cols), (1, 0, 2))
    my_kind = lax.all_to_all(my_kind, "fsdp", split_axis=0, concat_axis=0, tiled=True)
    core_pairs = [(j, j ^ 1) for j in range(lax.axis_size("img"))]
    other_kind = lax.ppermute(my_kind, "img", core_pairs)
    kv_weights = jnp.stack([my_kind, other_kind], 1)
    text_f = text_states.astype(jnp.float32)
    gained = (text_f * text_gain).astype(jnp.bfloat16)
    after_weights = my_kind[0, 0, 0].astype(jnp.float32) * 0.0
    stats = jnp.concatenate([jnp.sum(text_f * text_f, -1), final_gain], 0) + after_weights
    stats = gather_blocks(stats, "fsdp", parts)
    squares = jnp.sum(stats[:, :token_count], 0)
    full_gain = stats[:, token_count:].reshape(vis_width)
    query_cols = lax.psum_scatter(
        lax.dot_general(
            cross_query, gained, contract_first, preferred_element_type=jnp.float32
        ).astype(jnp.bfloat16),
        "fsdp",
        scatter_dimension=0,
        tiled=True,
    )
    full_patches = jnp.transpose(patch_blocks, (1, 2, 0, 3)).reshape(
        image_count, patch_count, vis_width
    )
    context = layer_norm(full_patches, context_gain).astype(jnp.bfloat16)
    latent_normed = layer_norm(latent_init, latent_gain).astype(jnp.bfloat16)
    res_q_rows = jnp.dot(latent_normed, res_query, preferred_element_type=jnp.float32).astype(
        jnp.bfloat16
    )
    res_q_rows = res_q_rows.reshape(latent_count, res_heads, RHD)
    ctx_keys = jnp.einsum(
        "npv,vk->npk", context, res_key, preferred_element_type=jnp.float32
    ).astype(jnp.bfloat16)
    ctx_values = jnp.einsum(
        "npv,vk->npk", context, res_value, preferred_element_type=jnp.float32
    ).astype(jnp.bfloat16)
    lat_keys = jnp.dot(latent_normed, res_key, preferred_element_type=jnp.float32).astype(
        jnp.bfloat16
    )
    lat_values = jnp.dot(latent_normed, res_value, preferred_element_type=jnp.float32).astype(
        jnp.bfloat16
    )
    joined_shape = (image_count, latent_count, res_cols)
    key_rows = jnp.concatenate([ctx_keys, jnp.broadcast_to(lat_keys[None], joined_shape)], 1)
    value_rows = jnp.concatenate([ctx_values, jnp.broadcast_to(lat_values[None], joined_shape)], 1)
    key_rows = key_rows.reshape(image_count, patch_count + latent_count, res_heads, RHD)
    value_rows = value_rows.reshape(image_count, patch_count + latent_count, res_heads, RHD)
    res_scores = jnp.einsum(
        "rhe,nkhe->nhrk", res_q_rows, key_rows, preferred_element_type=jnp.float32
    ) * RHD ** (-0.5)
    res_weights = jnp.exp(res_scores)
    res_weights = (res_weights / jnp.sum(res_weights, -1, keepdims=True)).astype(jnp.bfloat16)
    res_mixed = jnp.einsum(
        "nhrk,nkhe->nrhe", res_weights, value_rows, preferred_element_type=jnp.float32
    )
    res_mixed = res_mixed.astype(jnp.bfloat16).reshape(image_count * latent_count, res_cols)
    row_total = image_count * latent_count
    row_part = row_total // parts
    head_part = jnp.dot(res_mixed, res_out, preferred_element_type=jnp.float32).astype(jnp.bfloat16)
    head_part = lax.all_to_all(
        head_part.reshape(parts, row_part, vis_width), "fsdp", split_axis=0, concat_axis=0, tiled=True
    )
    my_rows = my_feature * row_part
    init_rows = lax.dynamic_slice_in_dim(latent_init, my_rows % latent_count, row_part, 0)
    latents = init_rows.astype(jnp.float32) + jnp.sum(head_part.astype(jnp.float32), 0)
    resampled_rows = layer_norm(latents, full_gain).astype(jnp.bfloat16)
    resampled = lax.all_to_all(
        jnp.transpose(resampled_rows.reshape(row_part, parts, feat_vis), (1, 0, 2)),
        "fsdp",
        split_axis=0,
        concat_axis=0,
        tiled=True,
    )
    per_image = resampled.reshape(image_count, latent_count * feat_vis)
    outgoing = pack_rows(per_image, wanted_images, my_shard, image_count, PAIR)
    incoming = lax.all_to_all(outgoing, "img", split_axis=0, concat_axis=0, tiled=True)
    slot_latents = unpack_rows(incoming, wanted_images, my_shard, image_count, PAIR).reshape(
        slot_count * latent_count, feat_vis
    )
    slot_blocks = gather_blocks(slot_latents, "fsdp", parts)
    slot_kv = jnp.einsum("brk,bskc->brsc", slot_blocks, kv_weights, preferred_element_type=jnp.float32)
    slot_kv = jnp.sum(lax.reduce_precision(slot_kv, exponent_bits=8, mantissa_bits=7), 0)
    slot_kv = slot_kv.astype(jnp.bfloat16).reshape(slot_count, latent_count, 2, cross_heads, HEAD)
    slot_keys = lax.dynamic_index_in_dim(slot_kv, my_core, 2, keepdims=False)
    slot_values = lax.dynamic_index_in_dim(slot_kv, 1 - my_core, 2, keepdims=False)
    token_scale = lax.rsqrt(squares / D + eps_rms)
    query_cols = (query_cols.astype(jnp.float32) * token_scale[None, :]).astype(jnp.bfloat16)
    query_heads = query_cols.reshape(cross_heads, HEAD, token_count)
    scores = jnp.einsum(
        "het,crhe->htcr", query_heads, slot_keys, preferred_element_type=jnp.float32
    ) * HEAD ** (-0.5)
    slot_hot = (token_slot[0][:, None] == jnp.arange(slot_count, dtype=jnp.int32)[None, :]).astype(
        jnp.float32
    )
    weights = jnp.exp(scores) * slot_hot[None, :, :, None]
    weights = (weights / jnp.sum(weights, axis=(2, 3), keepdims=True)).astype(jnp.bfloat16)
    attended = jnp.einsum(
        "htcr,crhe->het", weights, slot_values, preferred_element_type=jnp.float32
    )
    attended = attended.astype(jnp.bfloat16).reshape(head_cols, token_count)
    projected_cols = lax.psum_scatter(
        lax.dot_general(
            cross_out, attended, (((0,), (0,)), ((), ())), preferred_element_type=jnp.float32
        ).astype(jnp.bfloat16),
        "fsdp",
        scatter_dimension=0,
        tiled=True,
    ).astype(jnp.float32)
    projected = jnp.transpose(projected_cols)
    positions = jnp.arange(token_count, dtype=jnp.int32)
    live_mask = (positions < live_counts[0]).astype(jnp.float32)[:, None]
    return text_f + jnp.tanh(gate_scale) * projected * live_mask


def solution(mesh):
    placed = (
        P("img", "fsdp"),
        P("fsdp"),
        P("fsdp"),
        P("img"),
        P("img", None),
        P(),
        P("img", None, "fsdp"),
        P(),
        P(),
        P(),
        P(None, "fsdp"),
        P(None, "fsdp"),
        P(None, "fsdp"),
        P("fsdp", None),
        P("fsdp"),
        P("fsdp", None),
        P("fsdp", None),
        P("fsdp", None),
        P("fsdp", None),
    )
    return jax.shard_map(
        local, mesh=mesh, in_specs=placed, out_specs=P("img", "fsdp"), check_vma=False
    )
```

```python
import jax
import jax.numpy as jnp
from jax import lax
from jax.sharding import PartitionSpec as P

D = 8192
HEAD = 128
RHD = 96
PAIR = 2


eps_norm = 1e-05
eps_rms = 1e-06


def layer_norm(values, gain_vec):
    values = values.astype(jnp.float32)
    row_mean = jnp.mean(values, -1, keepdims=True)
    spread = jnp.mean(values * values, -1, keepdims=True) - row_mean * row_mean
    return (values - row_mean) * lax.rsqrt(spread + eps_norm) * gain_vec


def route_tables(wanted_images, per_owner, pair_slots):
    owners = wanted_images // per_owner
    slot_total = wanted_images.shape[1]
    positions = jnp.arange(slot_total, dtype=jnp.int32)
    before = (owners[:, :, None] == owners[:, None, :]) & (
        positions[None, None, :] < positions[None, :, None]
    )
    slot_rank = jnp.sum(before.astype(jnp.int32), axis=2)
    rank_hot = (
        slot_rank[:, :, None] == jnp.arange(pair_slots, dtype=jnp.int32)[None, None, :]
    ).astype(jnp.float32)
    return (owners, rank_hot)


def pack_rows(row_data, wanted_images, my_shard, per_owner, pair_slots):
    owners, rank_hot = route_tables(wanted_images, per_owner, pair_slots)
    is_mine = (owners == my_shard).astype(jnp.float32)
    local_hot = (
        (wanted_images % per_owner)[:, :, None]
        == jnp.arange(per_owner, dtype=jnp.int32)[None, None, :]
    ).astype(jnp.float32)
    picker = jnp.einsum("scp,sci->spi", rank_hot * is_mine[:, :, None], local_hot).astype(
        jnp.bfloat16
    )
    return jnp.einsum("spi,if->spf", picker, row_data, preferred_element_type=jnp.float32).astype(
        jnp.bfloat16
    )


def unpack_rows(received, wanted_images, my_shard, per_owner, pair_slots):
    owners, rank_hot = route_tables(wanted_images, per_owner, pair_slots)
    owner_row = lax.dynamic_slice_in_dim(owners, my_shard, 1, 0)[0]
    rank_row = lax.dynamic_slice_in_dim(rank_hot, my_shard, 1, 0)[0]
    source_hot = (
        owner_row[:, None] == jnp.arange(received.shape[0], dtype=jnp.int32)[None, :]
    ).astype(jnp.float32)
    taker = (source_hot[:, :, None] * rank_row[:, None, :]).astype(jnp.bfloat16)
    return jnp.einsum("cop,opf->cf", taker, received, preferred_element_type=jnp.float32).astype(
        jnp.bfloat16
    )


def gather_blocks(block, axis_name, parts):
    spread = jnp.broadcast_to(block[None], (parts,) + block.shape)
    return lax.all_to_all(spread, axis_name, split_axis=0, concat_axis=0, tiled=True)


def block_dot(rows, cols):
    contracted = jnp.einsum("brk,bkc->brc", rows, cols, preferred_element_type=jnp.float32)
    rounded = lax.reduce_precision(contracted, exponent_bits=8, mantissa_bits=7)
    return jnp.sum(rounded, 0)


def local(
    text_states,
    text_gain,
    gate_scale,
    live_counts,
    token_slot,
    wanted_images,
    patches,
    latent_init,
    context_gain,
    latent_gain,
    res_query,
    res_key,
    res_value,
    res_out,
    final_gain,
    cross_query,
    cross_key,
    cross_value,
    cross_out,
):
    my_feature = lax.axis_index("fsdp")
    my_shard = lax.axis_index("img")
    parts = lax.axis_size("fsdp")
    image_count = patches.shape[0]
    patch_count = patches.shape[1]
    feat_vis = patches.shape[2]
    latent_count = latent_init.shape[0]
    vis_width = latent_init.shape[1]
    res_cols = res_query.shape[1]
    res_heads = res_cols // RHD
    head_cols = cross_out.shape[0]
    token_count = text_states.shape[0]
    slot_count = wanted_images.shape[1]
    cross_heads = head_cols // HEAD
    contract_first = (((0,), (1,)), ((), ()))
    my_core = my_shard % 2
    kv_stack = jnp.stack([cross_key, cross_value], 0)
    my_kind = lax.dynamic_index_in_dim(kv_stack, my_core, 0, keepdims=False)
    my_kind = jnp.transpose(my_kind.reshape(feat_vis, parts, head_cols), (1, 0, 2))
    my_kind = lax.all_to_all(my_kind, "fsdp", split_axis=0, concat_axis=0, tiled=True)
    core_pairs = [(j, j ^ 1) for j in range(lax.axis_size("img"))]
    other_kind = lax.ppermute(my_kind, "img", core_pairs)
    kv_weights = jnp.stack([my_kind, other_kind], 1)
    text_f = text_states.astype(jnp.float32)
    gained = (text_f * text_gain).astype(jnp.bfloat16)
    after_weights = other_kind[0, 0, 0].astype(jnp.float32) * 0.0
    stats = jnp.concatenate([jnp.sum(text_f * text_f, -1), final_gain], 0) + after_weights
    stats = gather_blocks(stats, "fsdp", parts)
    squares = jnp.sum(stats[:, :token_count], 0)
    full_gain = stats[:, token_count:].reshape(vis_width)
    query_cols = lax.psum_scatter(
        lax.dot_general(
            cross_query, gained, contract_first, preferred_element_type=jnp.float32
        ).astype(jnp.bfloat16),
        "fsdp",
        scatter_dimension=0,
        tiled=True,
    )
    full_patches = lax.all_gather(patches, "fsdp", axis=2, tiled=True)
    context = layer_norm(full_patches, context_gain).astype(jnp.bfloat16)
    latent_normed = layer_norm(latent_init, latent_gain).astype(jnp.bfloat16)
    res_q_rows = jnp.dot(latent_normed, res_query, preferred_element_type=jnp.float32).astype(
        jnp.bfloat16
    )
    res_q_rows = res_q_rows.reshape(latent_count, res_heads, RHD)
    ctx_keys = jnp.einsum(
        "npv,vk->npk", context, res_key, preferred_element_type=jnp.float32
    ).astype(jnp.bfloat16)
    ctx_values = jnp.einsum(
        "npv,vk->npk", context, res_value, preferred_element_type=jnp.float32
    ).astype(jnp.bfloat16)
    lat_keys = jnp.dot(latent_normed, res_key, preferred_element_type=jnp.float32).astype(
        jnp.bfloat16
    )
    lat_values = jnp.dot(latent_normed, res_value, preferred_element_type=jnp.float32).astype(
        jnp.bfloat16
    )
    joined_shape = (image_count, latent_count, res_cols)
    key_rows = jnp.concatenate([ctx_keys, jnp.broadcast_to(lat_keys[None], joined_shape)], 1)
    value_rows = jnp.concatenate([ctx_values, jnp.broadcast_to(lat_values[None], joined_shape)], 1)
    key_rows = key_rows.reshape(image_count, patch_count + latent_count, res_heads, RHD)
    value_rows = value_rows.reshape(image_count, patch_count + latent_count, res_heads, RHD)
    res_scores = jnp.einsum(
        "rhe,nkhe->nhrk", res_q_rows, key_rows, preferred_element_type=jnp.float32
    ) * RHD ** (-0.5)
    res_weights = jnp.exp(res_scores)
    res_weights = (res_weights / jnp.sum(res_weights, -1, keepdims=True)).astype(jnp.bfloat16)
    res_mixed = jnp.einsum(
        "nhrk,nkhe->nrhe", res_weights, value_rows, preferred_element_type=jnp.float32
    )
    res_mixed = res_mixed.astype(jnp.bfloat16).reshape(image_count * latent_count, res_cols)
    row_total = image_count * latent_count
    row_part = row_total // parts
    head_part = jnp.dot(res_mixed, res_out, preferred_element_type=jnp.float32).astype(jnp.bfloat16)
    head_part = lax.all_to_all(
        head_part.reshape(parts, row_part, vis_width), "fsdp", split_axis=0, concat_axis=0, tiled=True
    )
    my_rows = my_feature * row_part
    init_rows = lax.dynamic_slice_in_dim(latent_init, my_rows % latent_count, row_part, 0)
    latents = init_rows.astype(jnp.float32) + jnp.sum(head_part.astype(jnp.float32), 0)
    resampled_rows = layer_norm(latents, full_gain).astype(jnp.bfloat16)
    resampled = lax.all_to_all(
        jnp.transpose(resampled_rows.reshape(row_part, parts, feat_vis), (1, 0, 2)),
        "fsdp",
        split_axis=0,
        concat_axis=0,
        tiled=True,
    )
    per_image = resampled.reshape(image_count, latent_count * feat_vis)
    outgoing = pack_rows(per_image, wanted_images, my_shard, image_count, PAIR)
    incoming = lax.all_to_all(outgoing, "img", split_axis=0, concat_axis=0, tiled=True)
    slot_latents = unpack_rows(incoming, wanted_images, my_shard, image_count, PAIR).reshape(
        slot_count * latent_count, feat_vis
    )
    slot_blocks = gather_blocks(slot_latents, "fsdp", parts)
    slot_kv = jnp.einsum("brk,bskc->brsc", slot_blocks, kv_weights, preferred_element_type=jnp.float32)
    slot_kv = jnp.sum(lax.reduce_precision(slot_kv, exponent_bits=8, mantissa_bits=7), 0)
    slot_kv = slot_kv.astype(jnp.bfloat16).reshape(slot_count, latent_count, 2, cross_heads, HEAD)
    slot_keys = lax.dynamic_index_in_dim(slot_kv, my_core, 2, keepdims=False)
    slot_values = lax.dynamic_index_in_dim(slot_kv, 1 - my_core, 2, keepdims=False)
    token_scale = lax.rsqrt(squares / D + eps_rms)
    query_cols = (query_cols.astype(jnp.float32) * token_scale[None, :]).astype(jnp.bfloat16)
    query_heads = query_cols.reshape(cross_heads, HEAD, token_count)
    scores = jnp.einsum(
        "het,crhe->htcr", query_heads, slot_keys, preferred_element_type=jnp.float32
    ) * HEAD ** (-0.5)
    slot_hot = (token_slot[0][:, None] == jnp.arange(slot_count, dtype=jnp.int32)[None, :]).astype(
        jnp.float32
    )
    weights = jnp.exp(scores) * slot_hot[None, :, :, None]
    weights = (weights / jnp.sum(weights, axis=(2, 3), keepdims=True)).astype(jnp.bfloat16)
    attended = jnp.einsum(
        "htcr,crhe->het", weights, slot_values, preferred_element_type=jnp.float32
    )
    attended = attended.astype(jnp.bfloat16).reshape(head_cols, token_count)
    projected_cols = lax.psum_scatter(
        lax.dot_general(
            cross_out, attended, (((0,), (0,)), ((), ())), preferred_element_type=jnp.float32
        ).astype(jnp.bfloat16),
        "fsdp",
        scatter_dimension=0,
        tiled=True,
    ).astype(jnp.float32)
    projected = jnp.transpose(projected_cols)
    positions = jnp.arange(token_count, dtype=jnp.int32)
    live_mask = (positions < live_counts[0]).astype(jnp.float32)[:, None]
    return text_f + jnp.tanh(gate_scale) * projected * live_mask


def solution(mesh):
    placed = (
        P("img", "fsdp"),
        P("fsdp"),
        P("fsdp"),
        P("img"),
        P("img", None),
        P(),
        P("img", None, "fsdp"),
        P(),
        P(),
        P(),
        P(None, "fsdp"),
        P(None, "fsdp"),
        P(None, "fsdp"),
        P("fsdp", None),
        P("fsdp"),
        P("fsdp", None),
        P("fsdp", None),
        P("fsdp", None),
        P("fsdp", None),
    )
    return jax.shard_map(
        local, mesh=mesh, in_specs=placed, out_specs=P("img", "fsdp"), check_vma=False
    )
```

```python
import jax
import jax.numpy as jnp
from jax import lax
from jax.sharding import PartitionSpec as P

D = 8192
HEAD = 128
RHD = 96
PAIR = 2


eps_norm = 1e-05
eps_rms = 1e-06


def layer_norm(values, gain_vec):
    values = values.astype(jnp.float32)
    row_mean = jnp.mean(values, -1, keepdims=True)
    spread = jnp.mean(values * values, -1, keepdims=True) - row_mean * row_mean
    return (values - row_mean) * lax.rsqrt(spread + eps_norm) * gain_vec


def route_tables(wanted_images, per_owner, pair_slots):
    owners = wanted_images // per_owner
    slot_total = wanted_images.shape[1]
    positions = jnp.arange(slot_total, dtype=jnp.int32)
    before = (owners[:, :, None] == owners[:, None, :]) & (
        positions[None, None, :] < positions[None, :, None]
    )
    slot_rank = jnp.sum(before.astype(jnp.int32), axis=2)
    rank_hot = (
        slot_rank[:, :, None] == jnp.arange(pair_slots, dtype=jnp.int32)[None, None, :]
    ).astype(jnp.float32)
    return (owners, rank_hot)


def pack_rows(row_data, wanted_images, my_shard, per_owner, pair_slots):
    owners, rank_hot = route_tables(wanted_images, per_owner, pair_slots)
    is_mine = (owners == my_shard).astype(jnp.float32)
    local_hot = (
        (wanted_images % per_owner)[:, :, None]
        == jnp.arange(per_owner, dtype=jnp.int32)[None, None, :]
    ).astype(jnp.float32)
    picker = jnp.einsum("scp,sci->spi", rank_hot * is_mine[:, :, None], local_hot).astype(
        jnp.bfloat16
    )
    return jnp.einsum("spi,if->spf", picker, row_data, preferred_element_type=jnp.float32).astype(
        jnp.bfloat16
    )


def unpack_rows(received, wanted_images, my_shard, per_owner, pair_slots):
    owners, rank_hot = route_tables(wanted_images, per_owner, pair_slots)
    owner_row = lax.dynamic_slice_in_dim(owners, my_shard, 1, 0)[0]
    rank_row = lax.dynamic_slice_in_dim(rank_hot, my_shard, 1, 0)[0]
    source_hot = (
        owner_row[:, None] == jnp.arange(received.shape[0], dtype=jnp.int32)[None, :]
    ).astype(jnp.float32)
    taker = (source_hot[:, :, None] * rank_row[:, None, :]).astype(jnp.bfloat16)
    return jnp.einsum("cop,opf->cf", taker, received, preferred_element_type=jnp.float32).astype(
        jnp.bfloat16
    )


def gather_blocks(block, axis_name, parts):
    spread = jnp.broadcast_to(block[None], (parts,) + block.shape)
    return lax.all_to_all(spread, axis_name, split_axis=0, concat_axis=0, tiled=True)


def block_dot(rows, cols):
    contracted = jnp.einsum("brk,bkc->brc", rows, cols, preferred_element_type=jnp.float32)
    rounded = lax.reduce_precision(contracted, exponent_bits=8, mantissa_bits=7)
    return jnp.sum(rounded, 0)


def local(
    text_states,
    text_gain,
    gate_scale,
    live_counts,
    token_slot,
    wanted_images,
    patches,
    latent_init,
    context_gain,
    latent_gain,
    res_query,
    res_key,
    res_value,
    res_out,
    final_gain,
    cross_query,
    cross_key,
    cross_value,
    cross_out,
):
    my_feature = lax.axis_index("fsdp")
    my_shard = lax.axis_index("img")
    parts = lax.axis_size("fsdp")
    image_count = patches.shape[0]
    patch_count = patches.shape[1]
    feat_vis = patches.shape[2]
    latent_count = latent_init.shape[0]
    vis_width = latent_init.shape[1]
    res_cols = res_query.shape[1]
    res_heads = res_cols // RHD
    head_cols = cross_out.shape[0]
    token_count = text_states.shape[0]
    slot_count = wanted_images.shape[1]
    cross_heads = head_cols // HEAD
    contract_first = (((0,), (1,)), ((), ()))
    my_core = my_shard % 2
    kv_stack = jnp.stack([cross_key, cross_value], 0)
    my_kind = lax.dynamic_index_in_dim(kv_stack, my_core, 0, keepdims=False)
    my_kind = jnp.transpose(my_kind.reshape(feat_vis, parts, head_cols), (1, 0, 2))
    my_kind = lax.all_to_all(my_kind, "fsdp", split_axis=0, concat_axis=0, tiled=True)
    core_pairs = [(j, j ^ 1) for j in range(lax.axis_size("img"))]
    other_kind = lax.ppermute(my_kind, "img", core_pairs)
    kv_weights = jnp.stack([my_kind, other_kind], 1)
    text_f = text_states.astype(jnp.float32)
    gained = (text_f * text_gain).astype(jnp.bfloat16)
    after_weights = my_kind[0, 0, 0].astype(jnp.float32) * 0.0
    stats = jnp.concatenate([jnp.sum(text_f * text_f, -1), final_gain], 0) + after_weights
    stats = gather_blocks(stats, "fsdp", parts)
    squares = jnp.sum(stats[:, :token_count], 0)
    full_gain = stats[:, token_count:].reshape(vis_width)
    query_cols = lax.psum_scatter(
        lax.dot_general(
            cross_query, gained, contract_first, preferred_element_type=jnp.float32
        ).astype(jnp.bfloat16),
        "fsdp",
        scatter_dimension=0,
        tiled=True,
    )
    full_patches = lax.all_gather(patches, "fsdp", axis=2, tiled=True)
    context = layer_norm(full_patches, context_gain).astype(jnp.bfloat16)
    latent_normed = layer_norm(latent_init, latent_gain).astype(jnp.bfloat16)
    res_q_rows = jnp.dot(latent_normed, res_query, preferred_element_type=jnp.float32).astype(
        jnp.bfloat16
    )
    res_q_rows = res_q_rows.reshape(latent_count, res_heads, RHD)
    ctx_keys = jnp.einsum(
        "npv,vk->npk", context, res_key, preferred_element_type=jnp.float32
    ).astype(jnp.bfloat16)
    ctx_values = jnp.einsum(
        "npv,vk->npk", context, res_value, preferred_element_type=jnp.float32
    ).astype(jnp.bfloat16)
    lat_keys = jnp.dot(latent_normed, res_key, preferred_element_type=jnp.float32).astype(
        jnp.bfloat16
    )
    lat_values = jnp.dot(latent_normed, res_value, preferred_element_type=jnp.float32).astype(
        jnp.bfloat16
    )
    joined_shape = (image_count, latent_count, res_cols)
    key_rows = jnp.concatenate([ctx_keys, jnp.broadcast_to(lat_keys[None], joined_shape)], 1)
    value_rows = jnp.concatenate([ctx_values, jnp.broadcast_to(lat_values[None], joined_shape)], 1)
    key_rows = key_rows.reshape(image_count, patch_count + latent_count, res_heads, RHD)
    value_rows = value_rows.reshape(image_count, patch_count + latent_count, res_heads, RHD)
    res_scores = jnp.einsum(
        "rhe,nkhe->nhrk", res_q_rows, key_rows, preferred_element_type=jnp.float32
    ) * RHD ** (-0.5)
    res_weights = jnp.exp(res_scores)
    res_weights = (res_weights / jnp.sum(res_weights, -1, keepdims=True)).astype(jnp.bfloat16)
    res_mixed = jnp.einsum(
        "nhrk,nkhe->nrhe", res_weights, value_rows, preferred_element_type=jnp.float32
    )
    res_mixed = res_mixed.astype(jnp.bfloat16).reshape(image_count * latent_count, res_cols)
    row_total = image_count * latent_count
    row_part = row_total // parts
    head_part = jnp.dot(res_mixed, res_out, preferred_element_type=jnp.float32).astype(jnp.bfloat16)
    head_part = lax.all_to_all(
        head_part.reshape(parts, row_part, vis_width), "fsdp", split_axis=0, concat_axis=0, tiled=True
    )
    my_rows = my_feature * row_part
    init_rows = lax.dynamic_slice_in_dim(latent_init, my_rows % latent_count, row_part, 0)
    latents = init_rows.astype(jnp.float32) + jnp.sum(head_part.astype(jnp.float32), 0)
    resampled_rows = layer_norm(latents, full_gain).astype(jnp.bfloat16)
    resampled = lax.all_to_all(
        jnp.transpose(resampled_rows.reshape(row_part, parts, feat_vis), (1, 0, 2)),
        "fsdp",
        split_axis=0,
        concat_axis=0,
        tiled=True,
    )
    per_image = resampled.reshape(image_count, latent_count * feat_vis)
    outgoing = pack_rows(per_image, wanted_images, my_shard, image_count, PAIR)
    incoming = lax.all_to_all(outgoing, "img", split_axis=0, concat_axis=0, tiled=True)
    slot_latents = unpack_rows(incoming, wanted_images, my_shard, image_count, PAIR).reshape(
        slot_count * latent_count, feat_vis
    )
    slot_blocks = gather_blocks(slot_latents, "fsdp", parts)
    slot_kv = jnp.einsum("brk,bskc->brsc", slot_blocks, kv_weights, preferred_element_type=jnp.float32)
    slot_kv = jnp.sum(lax.reduce_precision(slot_kv, exponent_bits=8, mantissa_bits=7), 0)
    slot_kv = slot_kv.astype(jnp.bfloat16).reshape(slot_count, latent_count, 2, cross_heads, HEAD)
    slot_keys = lax.dynamic_index_in_dim(slot_kv, my_core, 2, keepdims=False)
    slot_values = lax.dynamic_index_in_dim(slot_kv, 1 - my_core, 2, keepdims=False)
    token_scale = lax.rsqrt(squares / D + eps_rms) * HEAD ** (-0.5)
    query_heads = query_cols.reshape(cross_heads, HEAD, token_count)
    scores = jnp.einsum(
        "het,crhe->htcr", query_heads, slot_keys, preferred_element_type=jnp.float32
    ) * token_scale[None, :, None, None]
    slot_hot = (token_slot[0][:, None] == jnp.arange(slot_count, dtype=jnp.int32)[None, :]).astype(
        jnp.float32
    )
    weights = jnp.exp(scores) * slot_hot[None, :, :, None]
    weights = (weights / jnp.sum(weights, axis=(2, 3), keepdims=True)).astype(jnp.bfloat16)
    attended = jnp.einsum(
        "htcr,crhe->het", weights, slot_values, preferred_element_type=jnp.float32
    )
    attended = attended.astype(jnp.bfloat16).reshape(head_cols, token_count)
    projected_cols = lax.psum_scatter(
        lax.dot_general(
            cross_out, attended, (((0,), (0,)), ((), ())), preferred_element_type=jnp.float32
        ).astype(jnp.bfloat16),
        "fsdp",
        scatter_dimension=0,
        tiled=True,
    ).astype(jnp.float32)
    projected = jnp.transpose(projected_cols)
    positions = jnp.arange(token_count, dtype=jnp.int32)
    live_mask = (positions < live_counts[0]).astype(jnp.float32)[:, None]
    return text_f + jnp.tanh(gate_scale) * projected * live_mask


def solution(mesh):
    placed = (
        P("img", "fsdp"),
        P("fsdp"),
        P("fsdp"),
        P("img"),
        P("img", None),
        P(),
        P("img", None, "fsdp"),
        P(),
        P(),
        P(),
        P(None, "fsdp"),
        P(None, "fsdp"),
        P(None, "fsdp"),
        P("fsdp", None),
        P("fsdp"),
        P("fsdp", None),
        P("fsdp", None),
        P("fsdp", None),
        P("fsdp", None),
    )
    return jax.shard_map(
        local, mesh=mesh, in_specs=placed, out_specs=P("img", "fsdp"), check_vma=False
    )
```

```python
import jax
import jax.numpy as jnp
from jax import lax
from jax.sharding import PartitionSpec as P

D = 8192
HEAD = 128
RHD = 96
PAIR = 2


eps_norm = 1e-05
eps_rms = 1e-06


def layer_norm(values, gain_vec):
    values = values.astype(jnp.float32)
    row_mean = jnp.mean(values, -1, keepdims=True)
    spread = jnp.mean(values * values, -1, keepdims=True) - row_mean * row_mean
    return (values - row_mean) * lax.rsqrt(spread + eps_norm) * gain_vec


def route_tables(wanted_images, per_owner, pair_slots):
    owners = wanted_images // per_owner
    slot_total = wanted_images.shape[1]
    positions = jnp.arange(slot_total, dtype=jnp.int32)
    before = (owners[:, :, None] == owners[:, None, :]) & (
        positions[None, None, :] < positions[None, :, None]
    )
    slot_rank = jnp.sum(before.astype(jnp.int32), axis=2)
    rank_hot = (
        slot_rank[:, :, None] == jnp.arange(pair_slots, dtype=jnp.int32)[None, None, :]
    ).astype(jnp.float32)
    return (owners, rank_hot)


def pack_rows(row_data, wanted_images, my_shard, per_owner, pair_slots):
    owners, rank_hot = route_tables(wanted_images, per_owner, pair_slots)
    is_mine = (owners == my_shard).astype(jnp.float32)
    local_hot = (
        (wanted_images % per_owner)[:, :, None]
        == jnp.arange(per_owner, dtype=jnp.int32)[None, None, :]
    ).astype(jnp.float32)
    picker = jnp.einsum("scp,sci->spi", rank_hot * is_mine[:, :, None], local_hot).astype(
        jnp.bfloat16
    )
    return jnp.einsum("spi,if->spf", picker, row_data, preferred_element_type=jnp.float32).astype(
        jnp.bfloat16
    )


def unpack_rows(received, wanted_images, my_shard, per_owner, pair_slots):
    owners, rank_hot = route_tables(wanted_images, per_owner, pair_slots)
    owner_row = lax.dynamic_slice_in_dim(owners, my_shard, 1, 0)[0]
    rank_row = lax.dynamic_slice_in_dim(rank_hot, my_shard, 1, 0)[0]
    source_hot = (
        owner_row[:, None] == jnp.arange(received.shape[0], dtype=jnp.int32)[None, :]
    ).astype(jnp.float32)
    taker = (source_hot[:, :, None] * rank_row[:, None, :]).astype(jnp.bfloat16)
    return jnp.einsum("cop,opf->cf", taker, received, preferred_element_type=jnp.float32).astype(
        jnp.bfloat16
    )


def gather_blocks(block, axis_name, parts):
    spread = jnp.broadcast_to(block[None], (parts,) + block.shape)
    return lax.all_to_all(spread, axis_name, split_axis=0, concat_axis=0, tiled=True)


def block_dot(rows, cols):
    contracted = jnp.einsum("brk,bkc->brc", rows, cols, preferred_element_type=jnp.float32)
    rounded = lax.reduce_precision(contracted, exponent_bits=8, mantissa_bits=7)
    return jnp.sum(rounded, 0)


def local(
    text_states,
    text_gain,
    gate_scale,
    live_counts,
    token_slot,
    wanted_images,
    patches,
    latent_init,
    context_gain,
    latent_gain,
    res_query,
    res_key,
    res_value,
    res_out,
    final_gain,
    cross_query,
    cross_key,
    cross_value,
    cross_out,
):
    my_feature = lax.axis_index("fsdp")
    my_shard = lax.axis_index("img")
    parts = lax.axis_size("fsdp")
    image_count = patches.shape[0]
    patch_count = patches.shape[1]
    feat_vis = patches.shape[2]
    latent_count = latent_init.shape[0]
    vis_width = latent_init.shape[1]
    res_cols = res_query.shape[1]
    res_heads = res_cols // RHD
    head_cols = cross_out.shape[0]
    token_count = text_states.shape[0]
    slot_count = wanted_images.shape[1]
    cross_heads = head_cols // HEAD
    contract_first = (((0,), (1,)), ((), ()))
    my_core = my_shard % 2
    kv_stack = jnp.stack([cross_key, cross_value], 0)
    full_patches = lax.all_gather(patches, "fsdp", axis=2, tiled=True)
    after_patches = full_patches[0, 0, 0] * 0
    my_kind = lax.dynamic_index_in_dim(kv_stack, my_core, 0, keepdims=False) + after_patches
    my_kind = jnp.transpose(my_kind.reshape(feat_vis, parts, head_cols), (1, 0, 2))
    my_kind = lax.all_to_all(my_kind, "fsdp", split_axis=0, concat_axis=0, tiled=True)
    core_pairs = [(j, j ^ 1) for j in range(lax.axis_size("img"))]
    other_kind = lax.ppermute(my_kind, "img", core_pairs)
    kv_weights = jnp.stack([my_kind, other_kind], 1)
    text_f = text_states.astype(jnp.float32)
    gained = (text_f * text_gain).astype(jnp.bfloat16)
    after_weights = my_kind[0, 0, 0].astype(jnp.float32) * 0.0
    stats = jnp.concatenate([jnp.sum(text_f * text_f, -1), final_gain], 0) + after_weights
    stats = gather_blocks(stats, "fsdp", parts)
    squares = jnp.sum(stats[:, :token_count], 0)
    full_gain = stats[:, token_count:].reshape(vis_width)
    query_cols = lax.psum_scatter(
        lax.dot_general(
            cross_query, gained, contract_first, preferred_element_type=jnp.float32
        ).astype(jnp.bfloat16),
        "fsdp",
        scatter_dimension=0,
        tiled=True,
    )
    context = layer_norm(full_patches, context_gain).astype(jnp.bfloat16)
    latent_normed = layer_norm(latent_init, latent_gain).astype(jnp.bfloat16)
    res_q_rows = jnp.dot(latent_normed, res_query, preferred_element_type=jnp.float32).astype(
        jnp.bfloat16
    )
    res_q_rows = res_q_rows.reshape(latent_count, res_heads, RHD)
    ctx_keys = jnp.einsum(
        "npv,vk->npk", context, res_key, preferred_element_type=jnp.float32
    ).astype(jnp.bfloat16)
    ctx_values = jnp.einsum(
        "npv,vk->npk", context, res_value, preferred_element_type=jnp.float32
    ).astype(jnp.bfloat16)
    lat_keys = jnp.dot(latent_normed, res_key, preferred_element_type=jnp.float32).astype(
        jnp.bfloat16
    )
    lat_values = jnp.dot(latent_normed, res_value, preferred_element_type=jnp.float32).astype(
        jnp.bfloat16
    )
    joined_shape = (image_count, latent_count, res_cols)
    key_rows = jnp.concatenate([ctx_keys, jnp.broadcast_to(lat_keys[None], joined_shape)], 1)
    value_rows = jnp.concatenate([ctx_values, jnp.broadcast_to(lat_values[None], joined_shape)], 1)
    key_rows = key_rows.reshape(image_count, patch_count + latent_count, res_heads, RHD)
    value_rows = value_rows.reshape(image_count, patch_count + latent_count, res_heads, RHD)
    res_scores = jnp.einsum(
        "rhe,nkhe->nhrk", res_q_rows, key_rows, preferred_element_type=jnp.float32
    ) * RHD ** (-0.5)
    res_weights = jnp.exp(res_scores)
    res_weights = (res_weights / jnp.sum(res_weights, -1, keepdims=True)).astype(jnp.bfloat16)
    res_mixed = jnp.einsum(
        "nhrk,nkhe->nrhe", res_weights, value_rows, preferred_element_type=jnp.float32
    )
    res_mixed = res_mixed.astype(jnp.bfloat16).reshape(image_count * latent_count, res_cols)
    row_total = image_count * latent_count
    row_part = row_total // parts
    head_part = jnp.dot(res_mixed, res_out, preferred_element_type=jnp.float32).astype(jnp.bfloat16)
    head_part = lax.all_to_all(
        head_part.reshape(parts, row_part, vis_width), "fsdp", split_axis=0, concat_axis=0, tiled=True
    )
    my_rows = my_feature * row_part
    init_rows = lax.dynamic_slice_in_dim(latent_init, my_rows % latent_count, row_part, 0)
    latents = init_rows.astype(jnp.float32) + jnp.sum(head_part.astype(jnp.float32), 0)
    resampled_rows = layer_norm(latents, full_gain).astype(jnp.bfloat16)
    resampled = lax.all_to_all(
        jnp.transpose(resampled_rows.reshape(row_part, parts, feat_vis), (1, 0, 2)),
        "fsdp",
        split_axis=0,
        concat_axis=0,
        tiled=True,
    )
    per_image = resampled.reshape(image_count, latent_count * feat_vis)
    outgoing = pack_rows(per_image, wanted_images, my_shard, image_count, PAIR)
    incoming = lax.all_to_all(outgoing, "img", split_axis=0, concat_axis=0, tiled=True)
    slot_latents = unpack_rows(incoming, wanted_images, my_shard, image_count, PAIR).reshape(
        slot_count * latent_count, feat_vis
    )
    slot_blocks = gather_blocks(slot_latents, "fsdp", parts)
    slot_kv = jnp.einsum("brk,bskc->brsc", slot_blocks, kv_weights, preferred_element_type=jnp.float32)
    slot_kv = jnp.sum(lax.reduce_precision(slot_kv, exponent_bits=8, mantissa_bits=7), 0)
    slot_kv = slot_kv.astype(jnp.bfloat16).reshape(slot_count, latent_count, 2, cross_heads, HEAD)
    slot_keys = lax.dynamic_index_in_dim(slot_kv, my_core, 2, keepdims=False)
    slot_values = lax.dynamic_index_in_dim(slot_kv, 1 - my_core, 2, keepdims=False)
    token_scale = lax.rsqrt(squares / D + eps_rms)
    query_cols = (query_cols.astype(jnp.float32) * token_scale[None, :]).astype(jnp.bfloat16)
    query_heads = query_cols.reshape(cross_heads, HEAD, token_count)
    scores = jnp.einsum(
        "het,crhe->htcr", query_heads, slot_keys, preferred_element_type=jnp.float32
    ) * HEAD ** (-0.5)
    slot_hot = (token_slot[0][:, None] == jnp.arange(slot_count, dtype=jnp.int32)[None, :]).astype(
        jnp.float32
    )
    weights = jnp.exp(scores) * slot_hot[None, :, :, None]
    weights = (weights / jnp.sum(weights, axis=(2, 3), keepdims=True)).astype(jnp.bfloat16)
    attended = jnp.einsum(
        "htcr,crhe->het", weights, slot_values, preferred_element_type=jnp.float32
    )
    attended = attended.astype(jnp.bfloat16).reshape(head_cols, token_count)
    projected_cols = lax.psum_scatter(
        lax.dot_general(
            cross_out, attended, (((0,), (0,)), ((), ())), preferred_element_type=jnp.float32
        ).astype(jnp.bfloat16),
        "fsdp",
        scatter_dimension=0,
        tiled=True,
    ).astype(jnp.float32)
    projected = jnp.transpose(projected_cols)
    positions = jnp.arange(token_count, dtype=jnp.int32)
    live_mask = (positions < live_counts[0]).astype(jnp.float32)[:, None]
    return text_f + jnp.tanh(gate_scale) * projected * live_mask


def solution(mesh):
    placed = (
        P("img", "fsdp"),
        P("fsdp"),
        P("fsdp"),
        P("img"),
        P("img", None),
        P(),
        P("img", None, "fsdp"),
        P(),
        P(),
        P(),
        P(None, "fsdp"),
        P(None, "fsdp"),
        P(None, "fsdp"),
        P("fsdp", None),
        P("fsdp"),
        P("fsdp", None),
        P("fsdp", None),
        P("fsdp", None),
        P("fsdp", None),
    )
    return jax.shard_map(
        local, mesh=mesh, in_specs=placed, out_specs=P("img", "fsdp"), check_vma=False
    )
```

```python
import jax
import jax.numpy as jnp
from jax import lax
from jax.sharding import PartitionSpec as P

D = 8192
HEAD = 128
RHD = 96
PAIR = 2


eps_norm = 1e-05
eps_rms = 1e-06


def layer_norm(values, gain_vec):
    values = values.astype(jnp.float32)
    row_mean = jnp.mean(values, -1, keepdims=True)
    spread = jnp.mean(values * values, -1, keepdims=True) - row_mean * row_mean
    return (values - row_mean) * lax.rsqrt(spread + eps_norm) * gain_vec


def route_tables(wanted_images, per_owner, pair_slots):
    owners = wanted_images // per_owner
    slot_total = wanted_images.shape[1]
    positions = jnp.arange(slot_total, dtype=jnp.int32)
    before = (owners[:, :, None] == owners[:, None, :]) & (
        positions[None, None, :] < positions[None, :, None]
    )
    slot_rank = jnp.sum(before.astype(jnp.int32), axis=2)
    rank_hot = (
        slot_rank[:, :, None] == jnp.arange(pair_slots, dtype=jnp.int32)[None, None, :]
    ).astype(jnp.float32)
    return (owners, rank_hot)


def pack_rows(row_data, wanted_images, my_shard, per_owner, pair_slots):
    owners, rank_hot = route_tables(wanted_images, per_owner, pair_slots)
    is_mine = (owners == my_shard).astype(jnp.float32)
    local_hot = (
        (wanted_images % per_owner)[:, :, None]
        == jnp.arange(per_owner, dtype=jnp.int32)[None, None, :]
    ).astype(jnp.float32)
    picker = jnp.einsum("scp,sci->spi", rank_hot * is_mine[:, :, None], local_hot).astype(
        jnp.bfloat16
    )
    return jnp.einsum("spi,if->spf", picker, row_data, preferred_element_type=jnp.float32).astype(
        jnp.bfloat16
    )


def unpack_rows(received, wanted_images, my_shard, per_owner, pair_slots):
    owners, rank_hot = route_tables(wanted_images, per_owner, pair_slots)
    owner_row = lax.dynamic_slice_in_dim(owners, my_shard, 1, 0)[0]
    rank_row = lax.dynamic_slice_in_dim(rank_hot, my_shard, 1, 0)[0]
    source_hot = (
        owner_row[:, None] == jnp.arange(received.shape[0], dtype=jnp.int32)[None, :]
    ).astype(jnp.float32)
    taker = (source_hot[:, :, None] * rank_row[:, None, :]).astype(jnp.bfloat16)
    return jnp.einsum("cop,opf->cf", taker, received, preferred_element_type=jnp.float32).astype(
        jnp.bfloat16
    )


def gather_blocks(block, axis_name, parts):
    spread = jnp.broadcast_to(block[None], (parts,) + block.shape)
    return lax.all_to_all(spread, axis_name, split_axis=0, concat_axis=0, tiled=True)


def block_dot(rows, cols):
    contracted = jnp.einsum("brk,bkc->brc", rows, cols, preferred_element_type=jnp.float32)
    rounded = lax.reduce_precision(contracted, exponent_bits=8, mantissa_bits=7)
    return jnp.sum(rounded, 0)


def local(
    text_states,
    text_gain,
    gate_scale,
    live_counts,
    token_slot,
    wanted_images,
    patches,
    latent_init,
    context_gain,
    latent_gain,
    res_query,
    res_key,
    res_value,
    res_out,
    final_gain,
    cross_query,
    cross_key,
    cross_value,
    cross_out,
):
    my_feature = lax.axis_index("fsdp")
    my_shard = lax.axis_index("img")
    parts = lax.axis_size("fsdp")
    image_count = patches.shape[0]
    patch_count = patches.shape[1]
    feat_vis = patches.shape[2]
    latent_count = latent_init.shape[0]
    vis_width = latent_init.shape[1]
    res_cols = res_query.shape[1]
    res_heads = res_cols // RHD
    head_cols = cross_out.shape[0]
    token_count = text_states.shape[0]
    slot_count = wanted_images.shape[1]
    cross_heads = head_cols // HEAD
    contract_first = (((0,), (1,)), ((), ()))
    img_count = lax.axis_size("img")
    quarters = img_count // 2
    quarter_cols = head_cols // quarters
    kv_stack = jnp.stack([cross_key, cross_value], 0).reshape(
        2, feat_vis, parts, quarters, quarter_cols
    )
    my_kind = lax.dynamic_index_in_dim(kv_stack, my_shard % 2, 0, keepdims=False)
    my_part = lax.dynamic_index_in_dim(my_kind, my_shard // 2, 2, keepdims=False)
    my_part = lax.all_to_all(
        jnp.transpose(my_part, (1, 0, 2)), "fsdp", split_axis=0, concat_axis=0, tiled=True
    )
    all_parts = gather_blocks(my_part, "img", img_count).reshape(
        quarters, 2, parts, feat_vis, quarter_cols
    )
    kv_weights = jnp.transpose(all_parts, (2, 1, 3, 0, 4)).reshape(parts, 2, feat_vis, head_cols)
    text_f = text_states.astype(jnp.float32)
    gained = (text_f * text_gain).astype(jnp.bfloat16)
    after_weights = kv_weights[0, 0, 0, 0].astype(jnp.float32) * 0.0
    stats = jnp.concatenate([jnp.sum(text_f * text_f, -1), final_gain], 0) + after_weights
    stats = gather_blocks(stats, "fsdp", parts)
    squares = jnp.sum(stats[:, :token_count], 0)
    full_gain = stats[:, token_count:].reshape(vis_width)
    query_cols = lax.psum_scatter(
        lax.dot_general(
            cross_query, gained, contract_first, preferred_element_type=jnp.float32
        ).astype(jnp.bfloat16),
        "fsdp",
        scatter_dimension=0,
        tiled=True,
    )
    full_patches = lax.all_gather(patches, "fsdp", axis=2, tiled=True)
    context = layer_norm(full_patches, context_gain).astype(jnp.bfloat16)
    latent_normed = layer_norm(latent_init, latent_gain).astype(jnp.bfloat16)
    res_q_rows = jnp.dot(latent_normed, res_query, preferred_element_type=jnp.float32).astype(
        jnp.bfloat16
    )
    res_q_rows = res_q_rows.reshape(latent_count, res_heads, RHD)
    ctx_keys = jnp.einsum(
        "npv,vk->npk", context, res_key, preferred_element_type=jnp.float32
    ).astype(jnp.bfloat16)
    ctx_values = jnp.einsum(
        "npv,vk->npk", context, res_value, preferred_element_type=jnp.float32
    ).astype(jnp.bfloat16)
    lat_keys = jnp.dot(latent_normed, res_key, preferred_element_type=jnp.float32).astype(
        jnp.bfloat16
    )
    lat_values = jnp.dot(latent_normed, res_value, preferred_element_type=jnp.float32).astype(
        jnp.bfloat16
    )
    joined_shape = (image_count, latent_count, res_cols)
    key_rows = jnp.concatenate([ctx_keys, jnp.broadcast_to(lat_keys[None], joined_shape)], 1)
    value_rows = jnp.concatenate([ctx_values, jnp.broadcast_to(lat_values[None], joined_shape)], 1)
    key_rows = key_rows.reshape(image_count, patch_count + latent_count, res_heads, RHD)
    value_rows = value_rows.reshape(image_count, patch_count + latent_count, res_heads, RHD)
    res_scores = jnp.einsum(
        "rhe,nkhe->nhrk", res_q_rows, key_rows, preferred_element_type=jnp.float32
    ) * RHD ** (-0.5)
    res_weights = jnp.exp(res_scores)
    res_weights = (res_weights / jnp.sum(res_weights, -1, keepdims=True)).astype(jnp.bfloat16)
    res_mixed = jnp.einsum(
        "nhrk,nkhe->nrhe", res_weights, value_rows, preferred_element_type=jnp.float32
    )
    res_mixed = res_mixed.astype(jnp.bfloat16).reshape(image_count * latent_count, res_cols)
    row_total = image_count * latent_count
    row_part = row_total // parts
    head_part = jnp.dot(res_mixed, res_out, preferred_element_type=jnp.float32).astype(jnp.bfloat16)
    head_part = lax.all_to_all(
        head_part.reshape(parts, row_part, vis_width), "fsdp", split_axis=0, concat_axis=0, tiled=True
    )
    my_rows = my_feature * row_part
    init_rows = lax.dynamic_slice_in_dim(latent_init, my_rows % latent_count, row_part, 0)
    latents = init_rows.astype(jnp.float32) + jnp.sum(head_part.astype(jnp.float32), 0)
    resampled_rows = layer_norm(latents, full_gain).astype(jnp.bfloat16)
    resampled = lax.all_to_all(
        jnp.transpose(resampled_rows.reshape(row_part, parts, feat_vis), (1, 0, 2)),
        "fsdp",
        split_axis=0,
        concat_axis=0,
        tiled=True,
    )
    per_image = resampled.reshape(image_count, latent_count * feat_vis)
    outgoing = pack_rows(per_image, wanted_images, my_shard, image_count, PAIR)
    incoming = lax.all_to_all(outgoing, "img", split_axis=0, concat_axis=0, tiled=True)
    slot_latents = unpack_rows(incoming, wanted_images, my_shard, image_count, PAIR).reshape(
        slot_count * latent_count, feat_vis
    )
    slot_blocks = gather_blocks(slot_latents, "fsdp", parts)
    slot_kv = jnp.einsum("brk,bskc->brsc", slot_blocks, kv_weights, preferred_element_type=jnp.float32)
    slot_kv = jnp.sum(lax.reduce_precision(slot_kv, exponent_bits=8, mantissa_bits=7), 0)
    slot_kv = slot_kv.astype(jnp.bfloat16).reshape(slot_count, latent_count, 2, cross_heads, HEAD)
    slot_keys = slot_kv[:, :, 0]
    slot_values = slot_kv[:, :, 1]
    token_scale = lax.rsqrt(squares / D + eps_rms)
    query_cols = (query_cols.astype(jnp.float32) * token_scale[None, :]).astype(jnp.bfloat16)
    query_heads = query_cols.reshape(cross_heads, HEAD, token_count)
    scores = jnp.einsum(
        "het,crhe->htcr", query_heads, slot_keys, preferred_element_type=jnp.float32
    ) * HEAD ** (-0.5)
    slot_hot = (token_slot[0][:, None] == jnp.arange(slot_count, dtype=jnp.int32)[None, :]).astype(
        jnp.float32
    )
    weights = jnp.exp(scores) * slot_hot[None, :, :, None]
    weights = (weights / jnp.sum(weights, axis=(2, 3), keepdims=True)).astype(jnp.bfloat16)
    attended = jnp.einsum(
        "htcr,crhe->het", weights, slot_values, preferred_element_type=jnp.float32
    )
    attended = attended.astype(jnp.bfloat16).reshape(head_cols, token_count)
    projected_cols = lax.psum_scatter(
        lax.dot_general(
            cross_out, attended, (((0,), (0,)), ((), ())), preferred_element_type=jnp.float32
        ).astype(jnp.bfloat16),
        "fsdp",
        scatter_dimension=0,
        tiled=True,
    ).astype(jnp.float32)
    projected = jnp.transpose(projected_cols)
    positions = jnp.arange(token_count, dtype=jnp.int32)
    live_mask = (positions < live_counts[0]).astype(jnp.float32)[:, None]
    return text_f + jnp.tanh(gate_scale) * projected * live_mask


def solution(mesh):
    placed = (
        P("img", "fsdp"),
        P("fsdp"),
        P("fsdp"),
        P("img"),
        P("img", None),
        P(),
        P("img", None, "fsdp"),
        P(),
        P(),
        P(),
        P(None, "fsdp"),
        P(None, "fsdp"),
        P(None, "fsdp"),
        P("fsdp", None),
        P("fsdp"),
        P("fsdp", None),
        P("fsdp", None),
        P("fsdp", None),
        P("fsdp", None),
    )
    return jax.shard_map(
        local, mesh=mesh, in_specs=placed, out_specs=P("img", "fsdp"), check_vma=False
    )
```
